32 devices in a mesh: dom: 8 (over z, y), ka: 4 (over x, core).
Axes of the slice: x: 2, y: 2, z: 4, core: 2. Of those that a mesh axis runs over, the one named last changes fastest.
Arguments:
- cell_coordinates_frac: float32 [3, 49152], P(None, 'dom'), may hold values from 0 to 1
- site_strengths: bfloat16 [32, 49152], P(None, 'dom'), may hold values from -6 to 6
- miller_indices: int32 [3, 2048], P(None, 'ka'), may hold values from -11 to 16, as said below
- occupied_site_tally: int32 [8], P('dom'), may hold values from 3072 to 6144, as said below
- gaussian_spread: float32 [32], replicated, may hold values from 0.5 to 4
Outputs:
- potential: float32 [32, 49152], P(None, ('dom', 'ka'))
- forces: float32 [3, 49152], P(None, ('dom', 'ka'))
The draws below stay inside these ranges and needn't reach their ends.
Inputs may be any that keep to these rules, and one draw needn't show every extreme that they name: `miller_indices`: the vectors are distinct; h and k lie in -11 to 11 and l in 1 to 16, so none is zero; the extreme vectors (-11, -11, 1) and (11, 11, 16) occur. `occupied_site_tally`: some domain is full and some holds exactly half of its slots.
All inputs are finite; a program needn't handle non-finite values.
Results may differ from the reference program's by a relative error of at most 0.0044.
Values may be sent and summed in bfloat16 or wider, within the bound.
No kernel may reach another device: no remote copies, remote signals or barrier semaphores. Data moves between devices by JAX's collectives and lax.ppermute only.
A program may use at most 64 MiB of HBM per device.

```python
import math
import jax
import jax.numpy as jnp
from jax import lax

C = 32
ATOM_DEV = 6144
KVECS = 2048
ATOMS = 49152
N_DOM = 8


def draw_miller_indices(key, part):
    middle = jax.random.permutation(jax.random.fold_in(key, 11), 8462).astype(jnp.int32) + 1
    picked = middle[:KVECS - 2]
    index = jnp.concatenate([jnp.array([0, 8463], jnp.int32), picked], 0)
    first = index // 368 - 11
    second = index // 16 % 23 - 11
    third = index % 16 + 1
    return jnp.stack([first, second, third], 0).astype(jnp.int32)


def draw_occupied_site_tally(key, part):
    counts = jax.random.randint(jax.random.fold_in(key, 21), (N_DOM,), ATOM_DEV // 2, ATOM_DEV + 1)
    counts = counts.at[0].set(ATOM_DEV).at[1].set(ATOM_DEV // 2)
    return counts.astype(jnp.int32)


def levels(stream_key, dims, shards, smallest, high):
    def one(axis_at, parts):
        steps = jax.random.uniform(jax.random.fold_in(jax.random.fold_in(stream_key, 6), axis_at), (parts,), jnp.float32, smallest / len(shards), high / len(shards))
        return jnp.repeat(jnp.exp(steps), dims[axis_at] // parts).reshape((-1,) + (1,) * (len(dims) - axis_at - 1))

    loudness = one(*shards[0])
    for cut in shards[1:]:
        loudness = loudness * one(*cut)
    return loudness


def bell_draw(rng, extent, width, limit, split=(), dtype=jnp.bfloat16):
    level = levels(rng, extent, split, -0.22, 0.18) if split else 1.0
    result = jax.random.normal(rng, extent, jnp.float32) * width * level
    return jnp.minimum(jnp.maximum(result, -limit), limit).astype(dtype)


def setup_inputs(seed: int = 0) -> dict:
    key_list = jax.random.split(jax.random.key(seed), 6)
    return {
        "cell_coordinates_frac": jnp.clip(1.0 * jax.random.uniform(key_list[0], (3, ATOMS), jnp.float32) ** levels(key_list[0], (3, ATOMS), ((1, 8),), -0.2, 0.2), 0.0, 1.0),
        "site_strengths": bell_draw(key_list[1], (C, ATOMS), 1.0, 6.0, ((1, 8),)),
        "miller_indices": draw_miller_indices(jax.random.fold_in(key_list[5], 71), 0),
        "occupied_site_tally": draw_occupied_site_tally(jax.random.fold_in(key_list[5], 71), 0),
        "gaussian_spread": jnp.clip(jnp.exp(jax.random.uniform(key_list[4], (C,), jnp.float32, math.log(0.5), math.log(4.0))), 0.5, 4.0),
    }


two_pi = 6.283185307179586
box_length = 125.0

def phase_tables(cartesian_mode_vector, pos):
    angle = two_pi * (cartesian_mode_vector[0][:, None] * pos[0][None, :] + cartesian_mode_vector[1][:, None] * pos[1][None, :] + cartesian_mode_vector[2][:, None] * pos[2][None, :])
    return (jnp.cos(angle).astype(jnp.bfloat16), jnp.sin(angle).astype(jnp.bfloat16))

def reciprocal_filter_weight(s_cos, s_sin, cartesian_mode_vector, gaussian_spread, atoms_total):
    norm_sq = cartesian_mode_vector[0] * cartesian_mode_vector[0] + cartesian_mode_vector[1] * cartesian_mode_vector[1] + cartesian_mode_vector[2] * cartesian_mode_vector[2]
    scale = two_pi / box_length
    wavevector_norm_squared = scale * scale * norm_sq
    kernel = 2.0 * jnp.exp(-0.5 * (gaussian_spread * gaussian_spread)[:, None] * wavevector_norm_squared[None, :]) / norm_sq[None, :] / jnp.sqrt(jnp.float32(atoms_total))
    partial_first_term = kernel * s_cos
    partial_second_term = kernel * s_sin
    cos_side = jnp.concatenate([partial_first_term, -scale * cartesian_mode_vector[0] * partial_second_term, -scale * cartesian_mode_vector[1] * partial_second_term, -scale * cartesian_mode_vector[2] * partial_second_term], 0)
    sin_side = jnp.concatenate([partial_second_term, scale * cartesian_mode_vector[0] * partial_first_term, scale * cartesian_mode_vector[1] * partial_first_term, scale * cartesian_mode_vector[2] * partial_first_term], 0)
    return (cos_side.astype(jnp.bfloat16), sin_side.astype(jnp.bfloat16))

def masked_charges(charge_block, live_count):
    live = jnp.arange(charge_block.shape[1]) < live_count
    return (jnp.where(live[None, :], charge_block, jnp.zeros_like(charge_block)), live)

def reference(cell_coordinates_frac, site_strengths, miller_indices, occupied_site_tally, gaussian_spread):
    cartesian_mode_vector = miller_indices.astype(jnp.float32)
    position_blocks = cell_coordinates_frac.reshape(3, N_DOM, ATOM_DEV).transpose(1, 0, 2)
    charge_blocks = site_strengths.reshape(C, N_DOM, ATOM_DEV).transpose(1, 0, 2)
    high = lax.Precision.HIGHEST

    def add_domain(carry, items):
        pos, chg, live_count = items
        cos_table, sin_table = phase_tables(cartesian_mode_vector, pos)
        charge_live, live = masked_charges(chg, live_count)
        weights = charge_live.astype(jnp.float32)
        return ((carry[0] + jnp.dot(weights, cos_table.astype(jnp.float32).T, precision=high), carry[1] + jnp.dot(weights, sin_table.astype(jnp.float32).T, precision=high)), None)
    zeros = jnp.zeros((C, KVECS), jnp.float32)
    (s_cos, s_sin), _ = lax.scan(add_domain, (zeros, zeros), (position_blocks, charge_blocks, occupied_site_tally))
    cos_side, sin_side = reciprocal_filter_weight(s_cos, s_sin, cartesian_mode_vector, gaussian_spread, ATOMS)

    def per_domain(items):
        pos, chg, live_count = items
        cos_table, sin_table = phase_tables(cartesian_mode_vector, pos)
        charge_live, live = masked_charges(chg, live_count)
        field = jnp.dot(cos_side.astype(jnp.float32), cos_table.astype(jnp.float32), precision=high)
        field = field + jnp.dot(sin_side.astype(jnp.float32), sin_table.astype(jnp.float32), precision=high)
        weights = charge_live.astype(jnp.float32)
        potential = jnp.where(live[None, :], field[:C], jnp.zeros_like(field[:C]))
        forces = jnp.stack([lax.optimization_barrier(jnp.sum(weights * field[C * (1 + d):C * (2 + d)], 0)) for d in range(3)], 0)
        return (potential, forces)
    pots, frcs = lax.map(per_domain, (position_blocks, charge_blocks, occupied_site_tally))
    potential = pots.transpose(1, 0, 2).reshape(C, ATOMS)
    forces = frcs.transpose(1, 0, 2).reshape(3, ATOMS)
    return (potential, forces)
```

```python
import math

import jax
import jax.numpy as jnp
from jax import lax
from jax.sharding import PartitionSpec as P

two_pi = 6.283185307179586
box_length = 125.0

_COS_C = [(-1) ** n * two_pi ** (2 * n) / float(math.factorial(2 * n)) for n in range(6)]
_SIN_C = [(-1) ** n * two_pi ** (2 * n + 1) / float(math.factorial(2 * n + 1)) for n in range(6)]


def turns_cos_sin(t):
    r = t - jnp.round(t)
    q = jnp.round(4.0 * r)
    u = r - 0.25 * q
    u2 = u * u
    c = jnp.float32(_COS_C[5])
    for coef in _COS_C[4::-1]:
        c = c * u2 + jnp.float32(coef)
    s = jnp.float32(_SIN_C[5])
    for coef in _SIN_C[4::-1]:
        s = s * u2 + jnp.float32(coef)
    s = s * u
    cos_out = jnp.where(q == 0.0, c, jnp.where(q == 1.0, -s, jnp.where(q == -1.0, s, -c)))
    sin_out = jnp.where(q == 0.0, s, jnp.where(q == 1.0, c, jnp.where(q == -1.0, -c, -s)))
    return cos_out, sin_out


def reciprocal_filter_weight(s_cos, s_sin, cartesian_mode_vector, gaussian_spread, atoms_total):
    norm_sq = (
        cartesian_mode_vector[0] * cartesian_mode_vector[0]
        + cartesian_mode_vector[1] * cartesian_mode_vector[1]
        + cartesian_mode_vector[2] * cartesian_mode_vector[2]
    )
    scale = two_pi / box_length
    wavevector_norm_squared = scale * scale * norm_sq
    kernel = (
        2.0
        * jnp.exp(
            -0.5 * (gaussian_spread * gaussian_spread)[:, None] * wavevector_norm_squared[None, :]
        )
        / norm_sq[None, :]
        / jnp.sqrt(jnp.float32(atoms_total))
    )
    partial_first_term = kernel * s_cos
    partial_second_term = kernel * s_sin
    cos_side = jnp.concatenate(
        [
            partial_first_term,
            -scale * cartesian_mode_vector[0] * partial_second_term,
            -scale * cartesian_mode_vector[1] * partial_second_term,
            -scale * cartesian_mode_vector[2] * partial_second_term,
        ],
        0,
    )
    sin_side = jnp.concatenate(
        [
            partial_second_term,
            scale * cartesian_mode_vector[0] * partial_first_term,
            scale * cartesian_mode_vector[1] * partial_first_term,
            scale * cartesian_mode_vector[2] * partial_first_term,
        ],
        0,
    )
    return (cos_side.astype(jnp.bfloat16), sin_side.astype(jnp.bfloat16))


def butterfly_sum(x, axis, n):
    step = 1
    while step < n:
        x = x + lax.ppermute(x, axis, [(i, i ^ step) for i in range(n)])
        step *= 2
    return x


def halving_scatter(x, axis, n):
    rows_all = x.shape[1]
    rows = rows_all // n
    me = lax.axis_index(axis)
    held = x.reshape(x.shape[0], n, rows)
    step = 1
    while step < n:
        m = held.shape[1]
        pairs = held.reshape(held.shape[0], m // 2, 2, rows)
        bit = (me // step) % 2
        keep = jnp.where(bit == 0, pairs[:, :, 0], pairs[:, :, 1])
        send = jnp.where(bit == 0, pairs[:, :, 1], pairs[:, :, 0])
        held = keep + lax.ppermute(send, axis, [(i, i ^ step) for i in range(n)])
        step *= 2
    return held.reshape(held.shape[0], rows)


def make_local(n_dom, n_ka):
    def local(
        cell_coordinates_frac, site_strengths, miller_indices, occupied_site_tally, gaussian_spread
    ):
        channels = site_strengths.shape[0]
        n_local = cell_coordinates_frac.shape[1]
        atoms_total = n_local * n_dom
        live = jnp.arange(n_local) < occupied_site_tally[0]
        charge_live = jnp.where(live[None, :], site_strengths, jnp.zeros_like(site_strengths))
        cartesian_mode_vector = miller_indices.astype(jnp.float32)
        t = (
            cartesian_mode_vector[0][:, None] * cell_coordinates_frac[0][None, :]
            + cartesian_mode_vector[1][:, None] * cell_coordinates_frac[1][None, :]
            + cartesian_mode_vector[2][:, None] * cell_coordinates_frac[2][None, :]
        )
        cos_f, sin_f = turns_cos_sin(t)
        cos_table = cos_f.astype(jnp.bfloat16)
        sin_table = sin_f.astype(jnp.bfloat16)
        tensor_product = (((1,), (1,)), ((), ()))
        s_cos = lax.dot_general(
            charge_live, cos_table, tensor_product, preferred_element_type=jnp.float32
        )
        s_sin = lax.dot_general(
            charge_live, sin_table, tensor_product, preferred_element_type=jnp.float32
        )
        s_both = butterfly_sum(jnp.stack([s_cos, s_sin], 0), "dom", n_dom)
        cos_side, sin_side = reciprocal_filter_weight(
            s_both[0], s_both[1], cartesian_mode_vector, gaussian_spread, atoms_total
        )
        field = jnp.dot(cos_side, cos_table, preferred_element_type=jnp.float32)
        field = field + jnp.dot(sin_side, sin_table, preferred_element_type=jnp.float32)
        charge_f = charge_live.astype(jnp.float32)
        head = jnp.where(live[None, :], field[:channels], 0.0)
        force_rows = [
            jnp.sum(charge_f * field[channels * (1 + d) : channels * (2 + d)], 0, keepdims=True)
            for d in range(3)
        ]
        partial = jnp.concatenate([head] + force_rows, 0)
        own = halving_scatter(partial, "ka", n_ka)
        return (own[:channels], own[channels:])

    return local


def solution(mesh):
    placed = (P(None, "dom"), P(None, "dom"), P(None, "ka"), P("dom"), P())
    return jax.shard_map(
        make_local(mesh.shape["dom"], mesh.shape["ka"]),
        mesh=mesh,
        in_specs=placed,
        out_specs=(P(None, ("dom", "ka")), P(None, ("dom", "ka"))),
        check_vma=False,
    )
```

```python
import math

import jax
import jax.numpy as jnp
from jax import lax
from jax.sharding import PartitionSpec as P

two_pi = 6.283185307179586
box_length = 125.0

_COS_C = [(-1) ** n * two_pi ** (2 * n) / float(math.factorial(2 * n)) for n in range(6)]
_SIN_C = [(-1) ** n * two_pi ** (2 * n + 1) / float(math.factorial(2 * n + 1)) for n in range(6)]


def turns_cos_sin(t):
    r = t - jnp.floor(t + 0.5)
    q = jnp.floor(4.0 * r + 0.5)
    u = r - 0.25 * q
    u2 = u * u
    c = jnp.float32(_COS_C[4])
    for coef in _COS_C[3::-1]:
        c = c * u2 + jnp.float32(coef)
    s = jnp.float32(_SIN_C[4])
    for coef in _SIN_C[3::-1]:
        s = s * u2 + jnp.float32(coef)
    s = s * u
    odd = jnp.abs(q) == 1.0
    cos_mag = jnp.where(odd, s, c)
    sin_mag = jnp.where(odd, c, s)
    cos_out = jnp.where((q == 1.0) | (jnp.abs(q) == 2.0), -cos_mag, cos_mag)
    sin_out = jnp.where((q == -1.0) | (jnp.abs(q) == 2.0), -sin_mag, sin_mag)
    return cos_out, sin_out


def reciprocal_filter_weight(s_cos, s_sin, cartesian_mode_vector, gaussian_spread, atoms_total):
    norm_sq = (
        cartesian_mode_vector[0] * cartesian_mode_vector[0]
        + cartesian_mode_vector[1] * cartesian_mode_vector[1]
        + cartesian_mode_vector[2] * cartesian_mode_vector[2]
    )
    scale = two_pi / box_length
    wavevector_norm_squared = scale * scale * norm_sq
    kernel = (
        2.0
        * jnp.exp(
            -0.5 * (gaussian_spread * gaussian_spread)[:, None] * wavevector_norm_squared[None, :]
        )
        / norm_sq[None, :]
        / jnp.sqrt(jnp.float32(atoms_total))
    )
    partial_first_term = kernel * s_cos
    partial_second_term = kernel * s_sin
    cos_side = jnp.concatenate(
        [
            partial_first_term,
            -scale * cartesian_mode_vector[0] * partial_second_term,
            -scale * cartesian_mode_vector[1] * partial_second_term,
            -scale * cartesian_mode_vector[2] * partial_second_term,
        ],
        0,
    )
    sin_side = jnp.concatenate(
        [
            partial_second_term,
            scale * cartesian_mode_vector[0] * partial_first_term,
            scale * cartesian_mode_vector[1] * partial_first_term,
            scale * cartesian_mode_vector[2] * partial_first_term,
        ],
        0,
    )
    return (cos_side.astype(jnp.bfloat16), sin_side.astype(jnp.bfloat16))


def butterfly_sum(x, axis, n):
    step = 1
    while step < n:
        x = x + lax.ppermute(x, axis, [(i, i ^ step) for i in range(n)])
        step *= 2
    return x


def halving_scatter(x, axis, n):
    rows_all = x.shape[1]
    rows = rows_all // n
    me = lax.axis_index(axis)
    held = x.reshape(x.shape[0], n, rows)
    step = 1
    while step < n:
        m = held.shape[1]
        pairs = held.reshape(held.shape[0], m // 2, 2, rows)
        bit = (me // step) % 2
        keep = jnp.where(bit == 0, pairs[:, :, 0], pairs[:, :, 1])
        send = jnp.where(bit == 0, pairs[:, :, 1], pairs[:, :, 0])
        held = keep + lax.ppermute(send, axis, [(i, i ^ step) for i in range(n)])
        step *= 2
    return held.reshape(held.shape[0], rows)


def make_local(n_dom, n_ka):
    def local(
        cell_coordinates_frac, site_strengths, miller_indices, occupied_site_tally, gaussian_spread
    ):
        channels = site_strengths.shape[0]
        n_local = cell_coordinates_frac.shape[1]
        atoms_total = n_local * n_dom
        live = jnp.arange(n_local) < occupied_site_tally[0]
        charge_live = jnp.where(live[None, :], site_strengths, jnp.zeros_like(site_strengths))
        cartesian_mode_vector = miller_indices.astype(jnp.float32)
        t = (
            cartesian_mode_vector[0][:, None] * cell_coordinates_frac[0][None, :]
            + cartesian_mode_vector[1][:, None] * cell_coordinates_frac[1][None, :]
            + cartesian_mode_vector[2][:, None] * cell_coordinates_frac[2][None, :]
        )
        cos_f, sin_f = turns_cos_sin(t)
        cos_table = cos_f.astype(jnp.bfloat16)
        sin_table = sin_f.astype(jnp.bfloat16)
        cos_table, sin_table = lax.optimization_barrier((cos_table, sin_table))
        tensor_product = (((1,), (1,)), ((), ()))
        s_cos = lax.dot_general(
            charge_live, cos_table, tensor_product, preferred_element_type=jnp.float32
        )
        s_sin = lax.dot_general(
            charge_live, sin_table, tensor_product, preferred_element_type=jnp.float32
        )
        s_both = butterfly_sum(jnp.stack([s_cos, s_sin], 0), "dom", n_dom)
        cos_side, sin_side = reciprocal_filter_weight(
            s_both[0], s_both[1], cartesian_mode_vector, gaussian_spread, atoms_total
        )
        field = jnp.dot(cos_side, cos_table, preferred_element_type=jnp.float32)
        field = field + jnp.dot(sin_side, sin_table, preferred_element_type=jnp.float32)
        charge_f = charge_live.astype(jnp.float32)
        head = jnp.where(live[None, :], field[:channels], 0.0)
        force_rows = [
            jnp.sum(charge_f * field[channels * (1 + d) : channels * (2 + d)], 0, keepdims=True)
            for d in range(3)
        ]
        partial = jnp.concatenate([head] + force_rows, 0)
        own = halving_scatter(partial, "ka", n_ka)
        return (own[:channels], own[channels:])

    return local


def solution(mesh):
    placed = (P(None, "dom"), P(None, "dom"), P(None, "ka"), P("dom"), P())
    return jax.shard_map(
        make_local(mesh.shape["dom"], mesh.shape["ka"]),
        mesh=mesh,
        in_specs=placed,
        out_specs=(P(None, ("dom", "ka")), P(None, ("dom", "ka"))),
        check_vma=False,
    )
```

```python
import math

import jax
import jax.numpy as jnp
from jax import lax
from jax.sharding import PartitionSpec as P

two_pi = 6.283185307179586
box_length = 125.0

_COS_C = [(-1) ** n * two_pi ** (2 * n) / float(math.factorial(2 * n)) for n in range(6)]
_SIN_C = [(-1) ** n * two_pi ** (2 * n + 1) / float(math.factorial(2 * n + 1)) for n in range(6)]


def turns_cos_sin(t):
    r = t - jnp.floor(t + 0.5)
    q = jnp.floor(4.0 * r + 0.5)
    u = r - 0.25 * q
    u2 = u * u
    c = jnp.float32(_COS_C[4])
    for coef in _COS_C[3::-1]:
        c = c * u2 + jnp.float32(coef)
    s = jnp.float32(_SIN_C[4])
    for coef in _SIN_C[3::-1]:
        s = s * u2 + jnp.float32(coef)
    s = s * u
    odd = jnp.abs(q) == 1.0
    cos_mag = jnp.where(odd, s, c)
    sin_mag = jnp.where(odd, c, s)
    cos_out = jnp.where((q == 1.0) | (jnp.abs(q) == 2.0), -cos_mag, cos_mag)
    sin_out = jnp.where((q == -1.0) | (jnp.abs(q) == 2.0), -sin_mag, sin_mag)
    return cos_out, sin_out


def reciprocal_filter_weight(s_cos, s_sin, cartesian_mode_vector, gaussian_spread, atoms_total):
    norm_sq = (
        cartesian_mode_vector[0] * cartesian_mode_vector[0]
        + cartesian_mode_vector[1] * cartesian_mode_vector[1]
        + cartesian_mode_vector[2] * cartesian_mode_vector[2]
    )
    scale = two_pi / box_length
    wavevector_norm_squared = scale * scale * norm_sq
    kernel = (
        2.0
        * jnp.exp(
            -0.5 * (gaussian_spread * gaussian_spread)[:, None] * wavevector_norm_squared[None, :]
        )
        / norm_sq[None, :]
        / jnp.sqrt(jnp.float32(atoms_total))
    )
    partial_first_term = kernel * s_cos
    partial_second_term = kernel * s_sin
    cos_side = jnp.concatenate(
        [
            partial_first_term,
            -scale * cartesian_mode_vector[0] * partial_second_term,
            -scale * cartesian_mode_vector[1] * partial_second_term,
            -scale * cartesian_mode_vector[2] * partial_second_term,
        ],
        0,
    )
    sin_side = jnp.concatenate(
        [
            partial_second_term,
            scale * cartesian_mode_vector[0] * partial_first_term,
            scale * cartesian_mode_vector[1] * partial_first_term,
            scale * cartesian_mode_vector[2] * partial_first_term,
        ],
        0,
    )
    return (cos_side.astype(jnp.bfloat16), sin_side.astype(jnp.bfloat16))


def butterfly_sum(x, axis, n):
    step = 1
    while step < n:
        x = x + lax.ppermute(x, axis, [(i, i ^ step) for i in range(n)])
        step *= 2
    return x


def halving_scatter(x, axis, n):
    rows_all = x.shape[1]
    rows = rows_all // n
    me = lax.axis_index(axis)
    held = x.reshape(x.shape[0], n, rows)
    step = 1
    while step < n:
        m = held.shape[1]
        pairs = held.reshape(held.shape[0], m // 2, 2, rows)
        bit = (me // step) % 2
        keep = jnp.where(bit == 0, pairs[:, :, 0], pairs[:, :, 1])
        send = jnp.where(bit == 0, pairs[:, :, 1], pairs[:, :, 0])
        held = keep + lax.ppermute(send, axis, [(i, i ^ step) for i in range(n)])
        step *= 2
    return held.reshape(held.shape[0], rows)


def make_local(n_dom, n_ka):
    def local(
        cell_coordinates_frac, site_strengths, miller_indices, occupied_site_tally, gaussian_spread
    ):
        channels = site_strengths.shape[0]
        n_local = cell_coordinates_frac.shape[1]
        atoms_total = n_local * n_dom
        live = jnp.arange(n_local) < occupied_site_tally[0]
        charge_live = jnp.where(live[None, :], site_strengths, jnp.zeros_like(site_strengths))
        cartesian_mode_vector = miller_indices.astype(jnp.float32)
        n_k = cartesian_mode_vector.shape[1]
        chunk = 128 if n_k % 128 == 0 else n_k
        tensor_product = (((1,), (1,)), ((), ()))
        field = None
        pos = cell_coordinates_frac
        for start in range(0, n_k, chunk):
            mode = cartesian_mode_vector[:, start : start + chunk]
            t = (
                mode[0][:, None] * pos[0][None, :]
                + mode[1][:, None] * pos[1][None, :]
                + mode[2][:, None] * pos[2][None, :]
            )
            cos_f, sin_f = turns_cos_sin(t)
            cos_table = cos_f.astype(jnp.bfloat16)
            sin_table = sin_f.astype(jnp.bfloat16)
            cos_table, sin_table = lax.optimization_barrier((cos_table, sin_table))
            s_cos = lax.dot_general(
                charge_live, cos_table, tensor_product, preferred_element_type=jnp.float32
            )
            s_sin = lax.dot_general(
                charge_live, sin_table, tensor_product, preferred_element_type=jnp.float32
            )
            s_both = jnp.stack([s_cos, s_sin], 0)
            pos, s_both = lax.optimization_barrier((pos, s_both))
            s_both = butterfly_sum(s_both, "dom", n_dom)
            cos_side, sin_side = reciprocal_filter_weight(
                s_both[0], s_both[1], mode, gaussian_spread, atoms_total
            )
            part = jnp.dot(cos_side, cos_table, preferred_element_type=jnp.float32)
            part = part + jnp.dot(sin_side, sin_table, preferred_element_type=jnp.float32)
            field = part if field is None else field + part
        charge_f = charge_live.astype(jnp.float32)
        head = jnp.where(live[None, :], field[:channels], 0.0)
        force_rows = [
            jnp.sum(charge_f * field[channels * (1 + d) : channels * (2 + d)], 0, keepdims=True)
            for d in range(3)
        ]
        partial = jnp.concatenate([head] + force_rows, 0)
        own = halving_scatter(partial, "ka", n_ka)
        return (own[:channels], own[channels:])

    return local


def solution(mesh):
    placed = (P(None, "dom"), P(None, "dom"), P(None, "ka"), P("dom"), P())
    return jax.shard_map(
        make_local(mesh.shape["dom"], mesh.shape["ka"]),
        mesh=mesh,
        in_specs=placed,
        out_specs=(P(None, ("dom", "ka")), P(None, ("dom", "ka"))),
        check_vma=False,
    )
```

```python
import math

import jax
import jax.numpy as jnp
from jax import lax
from jax.experimental import pallas as pl
from jax.sharding import PartitionSpec as P

two_pi = 6.283185307179586
box_length = 125.0

_COS_C = [(-1) ** n * two_pi ** (2 * n) / float(math.factorial(2 * n)) for n in range(6)]
_SIN_C = [(-1) ** n * two_pi ** (2 * n + 1) / float(math.factorial(2 * n + 1)) for n in range(6)]


def turns_cos_sin(t):
    r = t - jnp.floor(t + 0.5)
    q = jnp.floor(4.0 * r + 0.5)
    u = r - 0.25 * q
    u2 = u * u
    c = jnp.float32(_COS_C[4])
    for coef in _COS_C[3::-1]:
        c = c * u2 + jnp.float32(coef)
    s = jnp.float32(_SIN_C[4])
    for coef in _SIN_C[3::-1]:
        s = s * u2 + jnp.float32(coef)
    s = s * u
    odd = jnp.abs(q) == 1.0
    cos_mag = jnp.where(odd, s, c)
    sin_mag = jnp.where(odd, c, s)
    cos_out = jnp.where((q == 1.0) | (jnp.abs(q) == 2.0), -cos_mag, cos_mag)
    sin_out = jnp.where((q == -1.0) | (jnp.abs(q) == 2.0), -sin_mag, sin_mag)
    return cos_out, sin_out


ROWS = 16
def table_kernel(mode_ref, pos_ref, q_ref, cos_ref, sin_ref, sc_ref, ss_ref):
    @pl.when(pl.program_id(0) == 0)
    def _():
        sc_ref[...] = jnp.zeros_like(sc_ref)
        ss_ref[...] = jnp.zeros_like(ss_ref)
    x = pos_ref[0:1, :]
    y = pos_ref[1:2, :]
    z = pos_ref[2:3, :]
    def body(g, carry):
        r0 = pl.multiple_of(g * ROWS, ROWS)
        m = mode_ref[pl.ds(r0, ROWS), :]
        t = m[:, 0:1] * x + m[:, 1:2] * y + m[:, 2:3] * z
        c, s = turns_cos_sin(t)
        cos_ref[pl.ds(r0, ROWS), :] = c.astype(jnp.bfloat16)
        sin_ref[pl.ds(r0, ROWS), :] = s.astype(jnp.bfloat16)
        return carry
    lax.fori_loop(0, cos_ref.shape[0] // ROWS, body, 0)
    nt = (((1,), (1,)), ((), ()))
    q = q_ref[...]
    sc_ref[...] += lax.dot_general(q, cos_ref[...], nt, preferred_element_type=jnp.float32)
    ss_ref[...] += lax.dot_general(q, sin_ref[...], nt, preferred_element_type=jnp.float32)

def tables_and_sums(mode_t, pos, charge, block=1536):
    n_k = mode_t.shape[0]
    n_at = pos.shape[1]
    ch = charge.shape[0]
    nb = n_at // block
    return pl.pallas_call(
        table_kernel,
        grid=(nb,),
        in_specs=[
            pl.BlockSpec((n_k, 3), lambda j: (0, 0)),
            pl.BlockSpec((3, block), lambda j: (0, j)),
            pl.BlockSpec((ch, block), lambda j: (0, j)),
        ],
        out_specs=[
            pl.BlockSpec((n_k, block), lambda j: (0, j)),
            pl.BlockSpec((n_k, block), lambda j: (0, j)),
            pl.BlockSpec((ch, n_k), lambda j: (0, 0)),
            pl.BlockSpec((ch, n_k), lambda j: (0, 0)),
        ],
        out_shape=[
            jax.ShapeDtypeStruct((n_k, n_at), jnp.bfloat16),
            jax.ShapeDtypeStruct((n_k, n_at), jnp.bfloat16),
            jax.ShapeDtypeStruct((ch, n_k), jnp.float32),
            jax.ShapeDtypeStruct((ch, n_k), jnp.float32),
        ],
    )(mode_t, pos, charge)


def reciprocal_filter_weight(s_cos, s_sin, cartesian_mode_vector, gaussian_spread, atoms_total):
    norm_sq = (
        cartesian_mode_vector[0] * cartesian_mode_vector[0]
        + cartesian_mode_vector[1] * cartesian_mode_vector[1]
        + cartesian_mode_vector[2] * cartesian_mode_vector[2]
    )
    scale = two_pi / box_length
    wavevector_norm_squared = scale * scale * norm_sq
    kernel = (
        2.0
        * jnp.exp(
            -0.5 * (gaussian_spread * gaussian_spread)[:, None] * wavevector_norm_squared[None, :]
        )
        / norm_sq[None, :]
        / jnp.sqrt(jnp.float32(atoms_total))
    )
    partial_first_term = kernel * s_cos
    partial_second_term = kernel * s_sin
    cos_side = jnp.concatenate(
        [
            partial_first_term,
            -scale * cartesian_mode_vector[0] * partial_second_term,
            -scale * cartesian_mode_vector[1] * partial_second_term,
            -scale * cartesian_mode_vector[2] * partial_second_term,
        ],
        0,
    )
    sin_side = jnp.concatenate(
        [
            partial_second_term,
            scale * cartesian_mode_vector[0] * partial_first_term,
            scale * cartesian_mode_vector[1] * partial_first_term,
            scale * cartesian_mode_vector[2] * partial_first_term,
        ],
        0,
    )
    return (cos_side.astype(jnp.bfloat16), sin_side.astype(jnp.bfloat16))


def butterfly_sum(x, axis, n):
    step = 1
    while step < n:
        x = x + lax.ppermute(x, axis, [(i, i ^ step) for i in range(n)])
        step *= 2
    return x


def halving_scatter(x, axis, n):
    rows_all = x.shape[1]
    rows = rows_all // n
    me = lax.axis_index(axis)
    held = x.reshape(x.shape[0], n, rows)
    step = 1
    while step < n:
        m = held.shape[1]
        pairs = held.reshape(held.shape[0], m // 2, 2, rows)
        bit = (me // step) % 2
        keep = jnp.where(bit == 0, pairs[:, :, 0], pairs[:, :, 1])
        send = jnp.where(bit == 0, pairs[:, :, 1], pairs[:, :, 0])
        held = keep + lax.ppermute(send, axis, [(i, i ^ step) for i in range(n)])
        step *= 2
    return held.reshape(held.shape[0], rows)


def make_local(n_dom, n_ka):
    def local(
        cell_coordinates_frac, site_strengths, miller_indices, occupied_site_tally, gaussian_spread
    ):
        channels = site_strengths.shape[0]
        n_local = cell_coordinates_frac.shape[1]
        atoms_total = n_local * n_dom
        live = jnp.arange(n_local) < occupied_site_tally[0]
        charge_live = jnp.where(live[None, :], site_strengths, jnp.zeros_like(site_strengths))
        cartesian_mode_vector = miller_indices.astype(jnp.float32)
        cos_table, sin_table, s_cos, s_sin = tables_and_sums(
            cartesian_mode_vector.T, cell_coordinates_frac, charge_live
        )
        s_both = butterfly_sum(jnp.stack([s_cos, s_sin], 0), "dom", n_dom)
        cos_side, sin_side = reciprocal_filter_weight(
            s_both[0], s_both[1], cartesian_mode_vector, gaussian_spread, atoms_total
        )
        field = jnp.dot(cos_side, cos_table, preferred_element_type=jnp.float32)
        field = field + jnp.dot(sin_side, sin_table, preferred_element_type=jnp.float32)
        charge_f = charge_live.astype(jnp.float32)
        head = jnp.where(live[None, :], field[:channels], 0.0)
        force_rows = [
            jnp.sum(charge_f * field[channels * (1 + d) : channels * (2 + d)], 0, keepdims=True)
            for d in range(3)
        ]
        partial = jnp.concatenate([head] + force_rows, 0)
        own = halving_scatter(partial, "ka", n_ka)
        return (own[:channels], own[channels:])

    return local


def solution(mesh):
    placed = (P(None, "dom"), P(None, "dom"), P(None, "ka"), P("dom"), P())
    return jax.shard_map(
        make_local(mesh.shape["dom"], mesh.shape["ka"]),
        mesh=mesh,
        in_specs=placed,
        out_specs=(P(None, ("dom", "ka")), P(None, ("dom", "ka"))),
        check_vma=False,
    )
```

```python
import math

import jax
import jax.numpy as jnp
from jax import lax
from jax.sharding import PartitionSpec as P

two_pi = 6.283185307179586
box_length = 125.0

_SIN_C = [(-1) ** n * math.pi ** (2 * n + 1) / float(math.factorial(2 * n + 1)) for n in range(6)]
_COS_C = [(-1) ** n * math.pi ** (2 * n) / float(math.factorial(2 * n)) for n in range(7)]


def turns_cos_sin(t):
    r = t - jnp.floor(t + 0.5)
    r2 = r * r
    s = jnp.float32(_SIN_C[-1])
    for coef in _SIN_C[-2::-1]:
        s = s * r2 + jnp.float32(coef)
    s = s * r
    c = jnp.float32(_COS_C[-1])
    for coef in _COS_C[-2::-1]:
        c = c * r2 + jnp.float32(coef)
    cos_out = 1.0 - 2.0 * (s * s)
    sin_out = 2.0 * (s * c)
    return cos_out, sin_out


def reciprocal_filter_weight(s_cos, s_sin, cartesian_mode_vector, gaussian_spread, atoms_total):
    norm_sq = (
        cartesian_mode_vector[0] * cartesian_mode_vector[0]
        + cartesian_mode_vector[1] * cartesian_mode_vector[1]
        + cartesian_mode_vector[2] * cartesian_mode_vector[2]
    )
    scale = two_pi / box_length
    wavevector_norm_squared = scale * scale * norm_sq
    kernel = (
        2.0
        * jnp.exp(
            -0.5 * (gaussian_spread * gaussian_spread)[:, None] * wavevector_norm_squared[None, :]
        )
        / norm_sq[None, :]
        / jnp.sqrt(jnp.float32(atoms_total))
    )
    partial_first_term = kernel * s_cos
    partial_second_term = kernel * s_sin
    cos_side = jnp.concatenate(
        [
            partial_first_term,
            -scale * cartesian_mode_vector[0] * partial_second_term,
            -scale * cartesian_mode_vector[1] * partial_second_term,
            -scale * cartesian_mode_vector[2] * partial_second_term,
        ],
        0,
    )
    sin_side = jnp.concatenate(
        [
            partial_second_term,
            scale * cartesian_mode_vector[0] * partial_first_term,
            scale * cartesian_mode_vector[1] * partial_first_term,
            scale * cartesian_mode_vector[2] * partial_first_term,
        ],
        0,
    )
    return (cos_side.astype(jnp.bfloat16), sin_side.astype(jnp.bfloat16))


def butterfly_sum(x, axis, n):
    step = 1
    while step < n:
        x = x + lax.ppermute(x, axis, [(i, i ^ step) for i in range(n)])
        step *= 2
    return x


def halving_scatter(x, axis, n):
    rows_all = x.shape[1]
    rows = rows_all // n
    me = lax.axis_index(axis)
    held = x.reshape(x.shape[0], n, rows)
    step = 1
    while step < n:
        m = held.shape[1]
        pairs = held.reshape(held.shape[0], m // 2, 2, rows)
        bit = (me // step) % 2
        keep = jnp.where(bit == 0, pairs[:, :, 0], pairs[:, :, 1])
        send = jnp.where(bit == 0, pairs[:, :, 1], pairs[:, :, 0])
        held = keep + lax.ppermute(send, axis, [(i, i ^ step) for i in range(n)])
        step *= 2
    return held.reshape(held.shape[0], rows)


def make_local(n_dom, n_ka):
    def local(
        cell_coordinates_frac, site_strengths, miller_indices, occupied_site_tally, gaussian_spread
    ):
        channels = site_strengths.shape[0]
        n_local = cell_coordinates_frac.shape[1]
        atoms_total = n_local * n_dom
        live = jnp.arange(n_local) < occupied_site_tally[0]
        charge_live = jnp.where(live[None, :], site_strengths, jnp.zeros_like(site_strengths))
        cartesian_mode_vector = miller_indices.astype(jnp.float32)
        t = (
            cartesian_mode_vector[0][:, None] * cell_coordinates_frac[0][None, :]
            + cartesian_mode_vector[1][:, None] * cell_coordinates_frac[1][None, :]
            + cartesian_mode_vector[2][:, None] * cell_coordinates_frac[2][None, :]
        )
        cos_f, sin_f = turns_cos_sin(t)
        cos_table = cos_f.astype(jnp.bfloat16)
        sin_table = sin_f.astype(jnp.bfloat16)
        cos_table, sin_table = lax.optimization_barrier((cos_table, sin_table))
        tensor_product = (((1,), (1,)), ((), ()))
        s_cos = lax.dot_general(
            charge_live, cos_table, tensor_product, preferred_element_type=jnp.float32
        )
        s_sin = lax.dot_general(
            charge_live, sin_table, tensor_product, preferred_element_type=jnp.float32
        )
        s_both = butterfly_sum(jnp.stack([s_cos, s_sin], 0), "dom", n_dom)
        cos_side, sin_side = reciprocal_filter_weight(
            s_both[0], s_both[1], cartesian_mode_vector, gaussian_spread, atoms_total
        )
        field = jnp.dot(cos_side, cos_table, preferred_element_type=jnp.float32)
        field = field + jnp.dot(sin_side, sin_table, preferred_element_type=jnp.float32)
        charge_f = charge_live.astype(jnp.float32)
        head = jnp.where(live[None, :], field[:channels], 0.0)
        force_rows = [
            jnp.sum(charge_f * field[channels * (1 + d) : channels * (2 + d)], 0, keepdims=True)
            for d in range(3)
        ]
        partial = jnp.concatenate([head] + force_rows, 0)
        own = halving_scatter(partial, "ka", n_ka)
        return (own[:channels], own[channels:])

    return local


def solution(mesh):
    placed = (P(None, "dom"), P(None, "dom"), P(None, "ka"), P("dom"), P())
    return jax.shard_map(
        make_local(mesh.shape["dom"], mesh.shape["ka"]),
        mesh=mesh,
        in_specs=placed,
        out_specs=(P(None, ("dom", "ka")), P(None, ("dom", "ka"))),
        check_vma=False,
    )
```

```python
import math

import jax
import jax.numpy as jnp
from jax import lax
from jax.sharding import PartitionSpec as P

two_pi = 6.283185307179586
box_length = 125.0

_SIN_C = [(-1) ** n * math.pi ** (2 * n + 1) / float(math.factorial(2 * n + 1)) for n in range(6)]
_COS_C = [(-1) ** n * math.pi ** (2 * n) / float(math.factorial(2 * n)) for n in range(7)]


def turns_cos_sin(t):
    r = t - jnp.floor(t + 0.5)
    r2 = r * r
    s = jnp.float32(_SIN_C[-1])
    for coef in _SIN_C[-2::-1]:
        s = s * r2 + jnp.float32(coef)
    s = s * r
    c = jnp.float32(_COS_C[-1])
    for coef in _COS_C[-2::-1]:
        c = c * r2 + jnp.float32(coef)
    cos_out = 1.0 - 2.0 * (s * s)
    sin_out = 2.0 * (s * c)
    return cos_out, sin_out


def reciprocal_filter_weight(s_cos, s_sin, cartesian_mode_vector, gaussian_spread, atoms_total):
    norm_sq = (
        cartesian_mode_vector[0] * cartesian_mode_vector[0]
        + cartesian_mode_vector[1] * cartesian_mode_vector[1]
        + cartesian_mode_vector[2] * cartesian_mode_vector[2]
    )
    scale = two_pi / box_length
    wavevector_norm_squared = scale * scale * norm_sq
    kernel = (
        2.0
        * jnp.exp(
            -0.5 * (gaussian_spread * gaussian_spread)[:, None] * wavevector_norm_squared[None, :]
        )
        / norm_sq[None, :]
        / jnp.sqrt(jnp.float32(atoms_total))
    )
    partial_first_term = kernel * s_cos
    partial_second_term = kernel * s_sin
    cos_side = jnp.concatenate(
        [
            partial_first_term,
            -scale * cartesian_mode_vector[0] * partial_second_term,
            -scale * cartesian_mode_vector[1] * partial_second_term,
            -scale * cartesian_mode_vector[2] * partial_second_term,
        ],
        0,
    )
    sin_side = jnp.concatenate(
        [
            partial_second_term,
            scale * cartesian_mode_vector[0] * partial_first_term,
            scale * cartesian_mode_vector[1] * partial_first_term,
            scale * cartesian_mode_vector[2] * partial_first_term,
        ],
        0,
    )
    return (cos_side.astype(jnp.bfloat16), sin_side.astype(jnp.bfloat16))


def butterfly_sum(x, axis, n):
    step = 1
    while step < n:
        x = x + lax.ppermute(x, axis, [(i, i ^ step) for i in range(n)])
        step *= 2
    return x


def halving_scatter(held, axis, n):
    me = lax.axis_index(axis)
    step = 1
    while step < n:
        m = held.shape[0]
        pairs = held.reshape(m // 2, 2, *held.shape[1:])
        bit = (me // step) % 2
        keep = jnp.where(bit == 0, pairs[:, 0], pairs[:, 1])
        send = jnp.where(bit == 0, pairs[:, 1], pairs[:, 0])
        held = keep + lax.ppermute(send, axis, [(i, i ^ step) for i in range(n)])
        step *= 2
    return held[0]


def make_local(n_dom, n_ka):
    def local(
        cell_coordinates_frac, site_strengths, miller_indices, occupied_site_tally, gaussian_spread
    ):
        channels = site_strengths.shape[0]
        n_local = cell_coordinates_frac.shape[1]
        atoms_total = n_local * n_dom
        live = jnp.arange(n_local) < occupied_site_tally[0]
        charge_live = jnp.where(live[None, :], site_strengths, jnp.zeros_like(site_strengths))
        cartesian_mode_vector = miller_indices.astype(jnp.float32)
        t = (
            cartesian_mode_vector[0][:, None] * cell_coordinates_frac[0][None, :]
            + cartesian_mode_vector[1][:, None] * cell_coordinates_frac[1][None, :]
            + cartesian_mode_vector[2][:, None] * cell_coordinates_frac[2][None, :]
        )
        cos_f, sin_f = turns_cos_sin(t)
        table = jnp.concatenate([cos_f, sin_f], 0).astype(jnp.bfloat16)
        table = lax.optimization_barrier(table)
        n_k = cartesian_mode_vector.shape[1]
        tensor_product = (((1,), (1,)), ((), ()))
        s_both = lax.dot_general(
            charge_live, table, tensor_product, preferred_element_type=jnp.float32
        )
        s_both = butterfly_sum(s_both.reshape(channels, 2, n_k), "dom", n_dom)
        cos_side, sin_side = reciprocal_filter_weight(
            s_both[:, 0], s_both[:, 1], cartesian_mode_vector, gaussian_spread, atoms_total
        )
        sides = jnp.concatenate([cos_side, sin_side], 1)
        field = jnp.dot(sides, table, preferred_element_type=jnp.float32)
        charge_f = charge_live.astype(jnp.float32)
        head = jnp.where(live[None, :], field[:channels], 0.0)
        force_rows = [
            jnp.sum(charge_f * field[channels * (1 + d) : channels * (2 + d)], 0, keepdims=True)
            for d in range(3)
        ]
        partial = jnp.concatenate([head] + force_rows, 0)
        rows = n_local // n_ka
        blocks = jnp.stack([partial[:, b * rows : (b + 1) * rows] for b in range(n_ka)], 0)
        own = halving_scatter(blocks, "ka", n_ka)
        return (own[:channels], own[channels:])

    return local


def solution(mesh):
    placed = (P(None, "dom"), P(None, "dom"), P(None, "ka"), P("dom"), P())
    return jax.shard_map(
        make_local(mesh.shape["dom"], mesh.shape["ka"]),
        mesh=mesh,
        in_specs=placed,
        out_specs=(P(None, ("dom", "ka")), P(None, ("dom", "ka"))),
        check_vma=False,
    )
```

```python
import math

import jax
import jax.numpy as jnp
from jax import lax
from jax.sharding import PartitionSpec as P

two_pi = 6.283185307179586
box_length = 125.0

_SIN_C = [(-1) ** n * math.pi ** (2 * n + 1) / float(math.factorial(2 * n + 1)) for n in range(6)]
_COS_C = [(-1) ** n * math.pi ** (2 * n) / float(math.factorial(2 * n)) for n in range(7)]


def turns_cos_sin(t):
    r = t - jnp.floor(t + 0.5)
    r2 = r * r
    s = jnp.float32(_SIN_C[-1])
    for coef in _SIN_C[-2::-1]:
        s = s * r2 + jnp.float32(coef)
    s = s * r
    c = jnp.float32(_COS_C[-1])
    for coef in _COS_C[-2::-1]:
        c = c * r2 + jnp.float32(coef)
    cos_out = 1.0 - 2.0 * (s * s)
    sin_out = 2.0 * (s * c)
    return cos_out, sin_out


def reciprocal_filter_weight(s_cos, s_sin, cartesian_mode_vector, gaussian_spread, atoms_total):
    norm_sq = (
        cartesian_mode_vector[0] * cartesian_mode_vector[0]
        + cartesian_mode_vector[1] * cartesian_mode_vector[1]
        + cartesian_mode_vector[2] * cartesian_mode_vector[2]
    )
    scale = two_pi / box_length
    wavevector_norm_squared = scale * scale * norm_sq
    kernel = (
        2.0
        * jnp.exp(
            -0.5 * (gaussian_spread * gaussian_spread)[:, None] * wavevector_norm_squared[None, :]
        )
        / norm_sq[None, :]
        / jnp.sqrt(jnp.float32(atoms_total))
    )
    partial_first_term = kernel * s_cos
    partial_second_term = kernel * s_sin
    cos_side = jnp.concatenate(
        [
            partial_first_term,
            -scale * cartesian_mode_vector[0] * partial_second_term,
            -scale * cartesian_mode_vector[1] * partial_second_term,
            -scale * cartesian_mode_vector[2] * partial_second_term,
        ],
        0,
    )
    sin_side = jnp.concatenate(
        [
            partial_second_term,
            scale * cartesian_mode_vector[0] * partial_first_term,
            scale * cartesian_mode_vector[1] * partial_first_term,
            scale * cartesian_mode_vector[2] * partial_first_term,
        ],
        0,
    )
    return (cos_side.astype(jnp.bfloat16), sin_side.astype(jnp.bfloat16))


def butterfly_sum(x, axis, n):
    step = 1
    while step < n:
        x = x + lax.ppermute(x, axis, [(i, i ^ step) for i in range(n)])
        step *= 2
    return x


def halving_scatter(held, axis, n):
    me = lax.axis_index(axis)
    step = 1
    while step < n:
        m = held.shape[0]
        pairs = held.reshape(m // 2, 2, *held.shape[1:])
        bit = (me // step) % 2
        keep = jnp.where(bit == 0, pairs[:, 0], pairs[:, 1])
        send = jnp.where(bit == 0, pairs[:, 1], pairs[:, 0])
        held = keep + lax.ppermute(send, axis, [(i, i ^ step) for i in range(n)])
        step *= 2
    return held[0]


def make_local(n_dom, n_ka):
    def local(
        cell_coordinates_frac, site_strengths, miller_indices, occupied_site_tally, gaussian_spread
    ):
        channels = site_strengths.shape[0]
        n_local = cell_coordinates_frac.shape[1]
        atoms_total = n_local * n_dom
        live = jnp.arange(n_local) < occupied_site_tally[0]
        charge_live = jnp.where(live[None, :], site_strengths, jnp.zeros_like(site_strengths))
        cartesian_mode_vector = miller_indices.astype(jnp.float32)
        t = (
            cartesian_mode_vector[0][:, None] * cell_coordinates_frac[0][None, :]
            + cartesian_mode_vector[1][:, None] * cell_coordinates_frac[1][None, :]
            + cartesian_mode_vector[2][:, None] * cell_coordinates_frac[2][None, :]
        )
        cos_f, sin_f = turns_cos_sin(t)
        cos_table = cos_f.astype(jnp.bfloat16)
        sin_table = sin_f.astype(jnp.bfloat16)
        cos_table, sin_table = lax.optimization_barrier((cos_table, sin_table))
        tensor_product = (((1,), (1,)), ((), ()))
        s_cos = lax.dot_general(
            charge_live, cos_table, tensor_product, preferred_element_type=jnp.float32
        )
        s_sin = lax.dot_general(
            charge_live, sin_table, tensor_product, preferred_element_type=jnp.float32
        )
        s_both = butterfly_sum(jnp.stack([s_cos, s_sin], 0), "dom", n_dom)
        cos_side, sin_side = reciprocal_filter_weight(
            s_both[0], s_both[1], cartesian_mode_vector, gaussian_spread, atoms_total
        )
        field = jnp.dot(cos_side, cos_table, preferred_element_type=jnp.float32)
        field = field + jnp.dot(sin_side, sin_table, preferred_element_type=jnp.float32)
        charge_f = charge_live.astype(jnp.float32)
        head = jnp.where(live[None, :], field[:channels], 0.0)
        force_rows = [
            jnp.sum(charge_f * field[channels * (1 + d) : channels * (2 + d)], 0, keepdims=True)
            for d in range(3)
        ]
        partial = jnp.concatenate([head] + force_rows, 0)
        rows = n_local // n_ka
        blocks = jnp.stack([partial[:, b * rows : (b + 1) * rows] for b in range(n_ka)], 0)
        own = halving_scatter(blocks, "ka", n_ka)
        return (own[:channels], own[channels:])

    return local


def solution(mesh):
    placed = (P(None, "dom"), P(None, "dom"), P(None, "ka"), P("dom"), P())
    return jax.shard_map(
        make_local(mesh.shape["dom"], mesh.shape["ka"]),
        mesh=mesh,
        in_specs=placed,
        out_specs=(P(None, ("dom", "ka")), P(None, ("dom", "ka"))),
        check_vma=False,
    )
```

```python
import math

import jax
import jax.numpy as jnp
from jax import lax
from jax.sharding import PartitionSpec as P

two_pi = 6.283185307179586
box_length = 125.0

_SIN_C = [3.1415926399240375, -5.167710053300693, 2.5500768575243145, -0.5982866957251158,
          0.0776479208030991]
_COS_C = [0.9999999525693762, -4.934792730768449, 4.058409142115622, -1.3318612751935888,
          0.2196570817648336]


def turns_cos_sin(t):
    r = t - jnp.floor(t + 0.5)
    r2 = r * r
    s = jnp.float32(_SIN_C[-1])
    for coef in _SIN_C[-2::-1]:
        s = s * r2 + jnp.float32(coef)
    s = s * r
    c = jnp.float32(_COS_C[-1])
    for coef in _COS_C[-2::-1]:
        c = c * r2 + jnp.float32(coef)
    cos_out = 1.0 - 2.0 * (s * s)
    sin_out = 2.0 * (s * c)
    return cos_out, sin_out


def reciprocal_filter_weight(s_cos, s_sin, cartesian_mode_vector, gaussian_spread, atoms_total):
    norm_sq = (
        cartesian_mode_vector[0] * cartesian_mode_vector[0]
        + cartesian_mode_vector[1] * cartesian_mode_vector[1]
        + cartesian_mode_vector[2] * cartesian_mode_vector[2]
    )
    scale = two_pi / box_length
    wavevector_norm_squared = scale * scale * norm_sq
    kernel = (
        2.0
        * jnp.exp(
            -0.5 * (gaussian_spread * gaussian_spread)[:, None] * wavevector_norm_squared[None, :]
        )
        / norm_sq[None, :]
        / jnp.sqrt(jnp.float32(atoms_total))
    )
    partial_first_term = kernel * s_cos
    partial_second_term = kernel * s_sin
    cos_side = jnp.concatenate(
        [
            partial_first_term,
            -scale * cartesian_mode_vector[0] * partial_second_term,
            -scale * cartesian_mode_vector[1] * partial_second_term,
            -scale * cartesian_mode_vector[2] * partial_second_term,
        ],
        0,
    )
    sin_side = jnp.concatenate(
        [
            partial_second_term,
            scale * cartesian_mode_vector[0] * partial_first_term,
            scale * cartesian_mode_vector[1] * partial_first_term,
            scale * cartesian_mode_vector[2] * partial_first_term,
        ],
        0,
    )
    return (cos_side.astype(jnp.bfloat16), sin_side.astype(jnp.bfloat16))


def butterfly_sum(x, axis, n):
    step = 1
    while step < n:
        x = x + lax.ppermute(x, axis, [(i, i ^ step) for i in range(n)])
        step *= 2
    return x


def halving_scatter(held, axis, n):
    me = lax.axis_index(axis)
    step = 1
    while step < n:
        m = held.shape[0]
        pairs = held.reshape(m // 2, 2, *held.shape[1:])
        bit = (me // step) % 2
        keep = jnp.where(bit == 0, pairs[:, 0], pairs[:, 1])
        send = jnp.where(bit == 0, pairs[:, 1], pairs[:, 0])
        held = keep + lax.ppermute(send, axis, [(i, i ^ step) for i in range(n)])
        step *= 2
    return held[0]


def make_local(n_dom, n_ka):
    def local(
        cell_coordinates_frac, site_strengths, miller_indices, occupied_site_tally, gaussian_spread
    ):
        channels = site_strengths.shape[0]
        n_local = cell_coordinates_frac.shape[1]
        atoms_total = n_local * n_dom
        live = jnp.arange(n_local) < occupied_site_tally[0]
        charge_live = jnp.where(live[None, :], site_strengths, jnp.zeros_like(site_strengths))
        cartesian_mode_vector = miller_indices.astype(jnp.float32)
        t = (
            cartesian_mode_vector[0][:, None] * cell_coordinates_frac[0][None, :]
            + cartesian_mode_vector[1][:, None] * cell_coordinates_frac[1][None, :]
            + cartesian_mode_vector[2][:, None] * cell_coordinates_frac[2][None, :]
        )
        cos_f, sin_f = turns_cos_sin(t)
        cos_table = cos_f.astype(jnp.bfloat16)
        sin_table = sin_f.astype(jnp.bfloat16)
        cos_table, sin_table = lax.optimization_barrier((cos_table, sin_table))
        tensor_product = (((1,), (1,)), ((), ()))
        s_cos = lax.dot_general(
            charge_live, cos_table, tensor_product, preferred_element_type=jnp.float32
        )
        s_sin = lax.dot_general(
            charge_live, sin_table, tensor_product, preferred_element_type=jnp.float32
        )
        s_both = butterfly_sum(jnp.stack([s_cos, s_sin], 0), "dom", n_dom)
        cos_side, sin_side = reciprocal_filter_weight(
            s_both[0], s_both[1], cartesian_mode_vector, gaussian_spread, atoms_total
        )
        field = jnp.dot(cos_side, cos_table, preferred_element_type=jnp.float32)
        field = field + jnp.dot(sin_side, sin_table, preferred_element_type=jnp.float32)
        charge_f = charge_live.astype(jnp.float32)
        head = jnp.where(live[None, :], field[:channels], 0.0)
        force_rows = [
            jnp.sum(charge_f * field[channels * (1 + d) : channels * (2 + d)], 0, keepdims=True)
            for d in range(3)
        ]
        partial = jnp.concatenate([head] + force_rows, 0)
        rows = n_local // n_ka
        blocks = jnp.stack([partial[:, b * rows : (b + 1) * rows] for b in range(n_ka)], 0)
        own = halving_scatter(blocks, "ka", n_ka)
        return (own[:channels], own[channels:])

    return local


def solution(mesh):
    placed = (P(None, "dom"), P(None, "dom"), P(None, "ka"), P("dom"), P())
    return jax.shard_map(
        make_local(mesh.shape["dom"], mesh.shape["ka"]),
        mesh=mesh,
        in_specs=placed,
        out_specs=(P(None, ("dom", "ka")), P(None, ("dom", "ka"))),
        check_vma=False,
    )
```

```python
import math

import jax
import jax.numpy as jnp
from jax import lax
from jax.sharding import PartitionSpec as P

two_pi = 6.283185307179586
box_length = 125.0

_SIN_C = [3.1415926399240375, -5.167710053300693, 2.5500768575243145, -0.5982866957251158,
          0.0776479208030991]
_COS_C = [0.9999999525693762, -4.934792730768449, 4.058409142115622, -1.3318612751935888,
          0.2196570817648336]
_ROOT2 = math.sqrt(2.0)


def turns_cos_sin(t):
    r = t - jnp.floor(t + 0.5)
    r2 = r * r
    s = jnp.float32(_SIN_C[-1] * _ROOT2)
    for coef in _SIN_C[-2::-1]:
        s = s * r2 + jnp.float32(coef * _ROOT2)
    s = s * r
    c = jnp.float32(_COS_C[-1] * _ROOT2)
    for coef in _COS_C[-2::-1]:
        c = c * r2 + jnp.float32(coef * _ROOT2)
    cos_out = 1.0 - s * s
    sin_out = s * c
    return cos_out, sin_out


def reciprocal_filter_weight(s_cos, s_sin, cartesian_mode_vector, gaussian_spread, atoms_total):
    norm_sq = (
        cartesian_mode_vector[0] * cartesian_mode_vector[0]
        + cartesian_mode_vector[1] * cartesian_mode_vector[1]
        + cartesian_mode_vector[2] * cartesian_mode_vector[2]
    )
    scale = two_pi / box_length
    wavevector_norm_squared = scale * scale * norm_sq
    kernel = (
        2.0
        * jnp.exp(
            -0.5 * (gaussian_spread * gaussian_spread)[:, None] * wavevector_norm_squared[None, :]
        )
        / norm_sq[None, :]
        / jnp.sqrt(jnp.float32(atoms_total))
    )
    partial_first_term = kernel * s_cos
    partial_second_term = kernel * s_sin
    cos_side = jnp.concatenate(
        [
            partial_first_term,
            -scale * cartesian_mode_vector[0] * partial_second_term,
            -scale * cartesian_mode_vector[1] * partial_second_term,
            -scale * cartesian_mode_vector[2] * partial_second_term,
        ],
        0,
    )
    sin_side = jnp.concatenate(
        [
            partial_second_term,
            scale * cartesian_mode_vector[0] * partial_first_term,
            scale * cartesian_mode_vector[1] * partial_first_term,
            scale * cartesian_mode_vector[2] * partial_first_term,
        ],
        0,
    )
    return (cos_side.astype(jnp.bfloat16), sin_side.astype(jnp.bfloat16))


def butterfly_sum(x, axis, n):
    step = 1
    while step < n:
        x = x + lax.ppermute(x, axis, [(i, i ^ step) for i in range(n)])
        step *= 2
    return x


def halving_scatter(held, axis, n):
    me = lax.axis_index(axis)
    step = 1
    while step < n:
        m = held.shape[0]
        pairs = held.reshape(m // 2, 2, *held.shape[1:])
        bit = (me // step) % 2
        keep = jnp.where(bit == 0, pairs[:, 0], pairs[:, 1])
        send = jnp.where(bit == 0, pairs[:, 1], pairs[:, 0])
        held = keep + lax.ppermute(send, axis, [(i, i ^ step) for i in range(n)])
        step *= 2
    return held[0]


def make_local(n_dom, n_ka):
    def local(
        cell_coordinates_frac, site_strengths, miller_indices, occupied_site_tally, gaussian_spread
    ):
        channels = site_strengths.shape[0]
        n_local = cell_coordinates_frac.shape[1]
        atoms_total = n_local * n_dom
        live = jnp.arange(n_local) < occupied_site_tally[0]
        charge_live = jnp.where(live[None, :], site_strengths, jnp.zeros_like(site_strengths))
        cartesian_mode_vector = miller_indices.astype(jnp.float32)
        t = (
            cartesian_mode_vector[0][:, None] * cell_coordinates_frac[0][None, :]
            + cartesian_mode_vector[1][:, None] * cell_coordinates_frac[1][None, :]
            + cartesian_mode_vector[2][:, None] * cell_coordinates_frac[2][None, :]
        )
        cos_f, sin_f = turns_cos_sin(t)
        cos_table = cos_f.astype(jnp.bfloat16)
        sin_table = sin_f.astype(jnp.bfloat16)
        cos_table, sin_table = lax.optimization_barrier((cos_table, sin_table))
        tensor_product = (((1,), (1,)), ((), ()))
        s_cos = lax.dot_general(
            charge_live, cos_table, tensor_product, preferred_element_type=jnp.float32
        )
        s_sin = lax.dot_general(
            charge_live, sin_table, tensor_product, preferred_element_type=jnp.float32
        )
        s_both = butterfly_sum(jnp.stack([s_cos, s_sin], 0), "dom", n_dom)
        cos_side, sin_side = reciprocal_filter_weight(
            s_both[0], s_both[1], cartesian_mode_vector, gaussian_spread, atoms_total
        )
        field = jnp.dot(cos_side, cos_table, preferred_element_type=jnp.float32)
        field = field + jnp.dot(sin_side, sin_table, preferred_element_type=jnp.float32)
        charge_f = charge_live.astype(jnp.float32)
        head = jnp.where(live[None, :], field[:channels], 0.0)
        force_rows = [
            jnp.sum(charge_f * field[channels * (1 + d) : channels * (2 + d)], 0, keepdims=True)
            for d in range(3)
        ]
        partial = jnp.concatenate([head] + force_rows, 0)
        rows = n_local // n_ka
        blocks = jnp.stack([partial[:, b * rows : (b + 1) * rows] for b in range(n_ka)], 0)
        own = halving_scatter(blocks, "ka", n_ka)
        return (own[:channels], own[channels:])

    return local


def solution(mesh):
    placed = (P(None, "dom"), P(None, "dom"), P(None, "ka"), P("dom"), P())
    return jax.shard_map(
        make_local(mesh.shape["dom"], mesh.shape["ka"]),
        mesh=mesh,
        in_specs=placed,
        out_specs=(P(None, ("dom", "ka")), P(None, ("dom", "ka"))),
        check_vma=False,
    )
```

```python
import math

import jax
import jax.numpy as jnp
from jax import lax
from jax.sharding import PartitionSpec as P

two_pi = 6.283185307179586
box_length = 125.0

_SIN_C = [3.1415926399240375, -5.167710053300693, 2.5500768575243145, -0.5982866957251158,
          0.0776479208030991]
_COS_C = [0.9999999525693762, -4.934792730768449, 4.058409142115622, -1.3318612751935888,
          0.2196570817648336]
_ROOT2 = math.sqrt(2.0)


def turns_cos_sin(t):
    r = t - jnp.floor(t + 0.5)
    r2 = r * r
    s = jnp.float32(_SIN_C[-1] * _ROOT2)
    for coef in _SIN_C[-2::-1]:
        s = s * r2 + jnp.float32(coef * _ROOT2)
    s = s * r
    c = jnp.float32(_COS_C[-1] * _ROOT2)
    for coef in _COS_C[-2::-1]:
        c = c * r2 + jnp.float32(coef * _ROOT2)
    cos_out = 1.0 - s * s
    sin_out = s * c
    return cos_out, sin_out


def reciprocal_filter_weight(s_cos, s_sin, cartesian_mode_vector, gaussian_spread, atoms_total):
    norm_sq = (
        cartesian_mode_vector[0] * cartesian_mode_vector[0]
        + cartesian_mode_vector[1] * cartesian_mode_vector[1]
        + cartesian_mode_vector[2] * cartesian_mode_vector[2]
    )
    scale = two_pi / box_length
    wavevector_norm_squared = scale * scale * norm_sq
    kernel = (
        2.0
        * jnp.exp(
            -0.5 * (gaussian_spread * gaussian_spread)[:, None] * wavevector_norm_squared[None, :]
        )
        / norm_sq[None, :]
        / jnp.sqrt(jnp.float32(atoms_total))
    )
    partial_first_term = kernel * s_cos
    partial_second_term = kernel * s_sin
    cos_side = jnp.concatenate(
        [
            partial_first_term,
            -scale * cartesian_mode_vector[0] * partial_second_term,
            -scale * cartesian_mode_vector[1] * partial_second_term,
            -scale * cartesian_mode_vector[2] * partial_second_term,
        ],
        0,
    )
    sin_side = jnp.concatenate(
        [
            partial_second_term,
            scale * cartesian_mode_vector[0] * partial_first_term,
            scale * cartesian_mode_vector[1] * partial_first_term,
            scale * cartesian_mode_vector[2] * partial_first_term,
        ],
        0,
    )
    return (cos_side.astype(jnp.bfloat16), sin_side.astype(jnp.bfloat16))


def butterfly_sum(x, axis, n):
    step = 1
    while step < n:
        x = x + lax.ppermute(x, axis, [(i, i ^ step) for i in range(n)])
        step *= 2
    return x


def halving_scatter(held, axis, n):
    me = lax.axis_index(axis)
    step = 1
    while step < n:
        m = held.shape[0]
        pairs = held.reshape(m // 2, 2, *held.shape[1:])
        bit = (me // step) % 2
        keep = jnp.where(bit == 0, pairs[:, 0], pairs[:, 1])
        send = jnp.where(bit == 0, pairs[:, 1], pairs[:, 0])
        pairs_list = [(i, i ^ step) for i in range(n)]
        if step >= 2:
            recv = lax.ppermute(send.astype(jnp.bfloat16), axis, pairs_list).astype(jnp.float32)
        else:
            recv = lax.ppermute(send, axis, pairs_list)
        held = keep + recv
        step *= 2
    return held[0]


def make_local(n_dom, n_ka):
    def local(
        cell_coordinates_frac, site_strengths, miller_indices, occupied_site_tally, gaussian_spread
    ):
        channels = site_strengths.shape[0]
        n_local = cell_coordinates_frac.shape[1]
        atoms_total = n_local * n_dom
        live = jnp.arange(n_local) < occupied_site_tally[0]
        charge_live = jnp.where(live[None, :], site_strengths, jnp.zeros_like(site_strengths))
        cartesian_mode_vector = miller_indices.astype(jnp.float32)
        t = (
            cartesian_mode_vector[0][:, None] * cell_coordinates_frac[0][None, :]
            + cartesian_mode_vector[1][:, None] * cell_coordinates_frac[1][None, :]
            + cartesian_mode_vector[2][:, None] * cell_coordinates_frac[2][None, :]
        )
        cos_f, sin_f = turns_cos_sin(t)
        cos_table = cos_f.astype(jnp.bfloat16)
        sin_table = sin_f.astype(jnp.bfloat16)
        cos_table, sin_table = lax.optimization_barrier((cos_table, sin_table))
        tensor_product = (((1,), (1,)), ((), ()))
        s_cos = lax.dot_general(
            charge_live, cos_table, tensor_product, preferred_element_type=jnp.float32
        )
        s_sin = lax.dot_general(
            charge_live, sin_table, tensor_product, preferred_element_type=jnp.float32
        )
        s_both = butterfly_sum(jnp.stack([s_cos, s_sin], 0), "dom", n_dom)
        cos_side, sin_side = reciprocal_filter_weight(
            s_both[0], s_both[1], cartesian_mode_vector, gaussian_spread, atoms_total
        )
        field = jnp.dot(cos_side, cos_table, preferred_element_type=jnp.float32)
        field = field + jnp.dot(sin_side, sin_table, preferred_element_type=jnp.float32)
        charge_f = charge_live.astype(jnp.float32)
        head = jnp.where(live[None, :], field[:channels], 0.0)
        force_rows = [
            jnp.sum(charge_f * field[channels * (1 + d) : channels * (2 + d)], 0, keepdims=True)
            for d in range(3)
        ]
        partial = jnp.concatenate([head] + force_rows, 0)
        rows = n_local // n_ka
        blocks = jnp.stack([partial[:, b * rows : (b + 1) * rows] for b in range(n_ka)], 0)
        own = halving_scatter(blocks, "ka", n_ka)
        return (own[:channels], own[channels:])

    return local


def solution(mesh):
    placed = (P(None, "dom"), P(None, "dom"), P(None, "ka"), P("dom"), P())
    return jax.shard_map(
        make_local(mesh.shape["dom"], mesh.shape["ka"]),
        mesh=mesh,
        in_specs=placed,
        out_specs=(P(None, ("dom", "ka")), P(None, ("dom", "ka"))),
        check_vma=False,
    )
```

```python
import math

import jax
import jax.numpy as jnp
from jax import lax
from jax.sharding import PartitionSpec as P

two_pi = 6.283185307179586
box_length = 125.0

_SIN_C = [3.1415926399240375, -5.167710053300693, 2.5500768575243145, -0.5982866957251158,
          0.0776479208030991]
_COS_C = [0.9999999525693762, -4.934792730768449, 4.058409142115622, -1.3318612751935888,
          0.2196570817648336]
_ROOT2 = math.sqrt(2.0)


def turns_cos_sin(t):
    r = t - jnp.floor(t + 0.5)
    r2 = r * r
    s = jnp.float32(_SIN_C[-1] * _ROOT2)
    for coef in _SIN_C[-2::-1]:
        s = s * r2 + jnp.float32(coef * _ROOT2)
    s = s * r
    c = jnp.float32(_COS_C[-1] * _ROOT2)
    for coef in _COS_C[-2::-1]:
        c = c * r2 + jnp.float32(coef * _ROOT2)
    cos_out = 1.0 - s * s
    sin_out = s * c
    return cos_out, sin_out


def reciprocal_filter_weight(s_cos, s_sin, cartesian_mode_vector, gaussian_spread, atoms_total):
    norm_sq = (
        cartesian_mode_vector[0] * cartesian_mode_vector[0]
        + cartesian_mode_vector[1] * cartesian_mode_vector[1]
        + cartesian_mode_vector[2] * cartesian_mode_vector[2]
    )
    scale = two_pi / box_length
    wavevector_norm_squared = scale * scale * norm_sq
    kernel = (
        2.0
        * jnp.exp(
            -0.5 * (gaussian_spread * gaussian_spread)[:, None] * wavevector_norm_squared[None, :]
        )
        / norm_sq[None, :]
        / jnp.sqrt(jnp.float32(atoms_total))
    )
    partial_first_term = kernel * s_cos
    partial_second_term = kernel * s_sin
    cos_side = jnp.concatenate(
        [
            partial_first_term,
            -scale * cartesian_mode_vector[0] * partial_second_term,
            -scale * cartesian_mode_vector[1] * partial_second_term,
            -scale * cartesian_mode_vector[2] * partial_second_term,
        ],
        0,
    )
    sin_side = jnp.concatenate(
        [
            partial_second_term,
            scale * cartesian_mode_vector[0] * partial_first_term,
            scale * cartesian_mode_vector[1] * partial_first_term,
            scale * cartesian_mode_vector[2] * partial_first_term,
        ],
        0,
    )
    return (cos_side.astype(jnp.bfloat16), sin_side.astype(jnp.bfloat16))


def butterfly_sum(x, axis, n):
    step = n // 2
    while step >= 1:
        x = x + lax.ppermute(x, axis, [(i, i ^ step) for i in range(n)])
        step //= 2
    return x


def halving_scatter(held, axis, n):
    me = lax.axis_index(axis)
    step = 1
    while step < n:
        m = held.shape[0]
        pairs = held.reshape(m // 2, 2, *held.shape[1:])
        bit = (me // step) % 2
        keep = jnp.where(bit == 0, pairs[:, 0], pairs[:, 1])
        send = jnp.where(bit == 0, pairs[:, 1], pairs[:, 0])
        pairs_list = [(i, i ^ step) for i in range(n)]
        if step >= 2:
            recv = lax.ppermute(send.astype(jnp.bfloat16), axis, pairs_list).astype(jnp.float32)
        else:
            recv = lax.ppermute(send, axis, pairs_list)
        held = keep + recv
        step *= 2
    return held[0]


def make_local(n_dom, n_ka):
    def local(
        cell_coordinates_frac, site_strengths, miller_indices, occupied_site_tally, gaussian_spread
    ):
        channels = site_strengths.shape[0]
        n_local = cell_coordinates_frac.shape[1]
        atoms_total = n_local * n_dom
        live = jnp.arange(n_local) < occupied_site_tally[0]
        charge_live = jnp.where(live[None, :], site_strengths, jnp.zeros_like(site_strengths))
        cartesian_mode_vector = miller_indices.astype(jnp.float32)
        t = (
            cartesian_mode_vector[0][:, None] * cell_coordinates_frac[0][None, :]
            + cartesian_mode_vector[1][:, None] * cell_coordinates_frac[1][None, :]
            + cartesian_mode_vector[2][:, None] * cell_coordinates_frac[2][None, :]
        )
        cos_f, sin_f = turns_cos_sin(t)
        cos_table = cos_f.astype(jnp.bfloat16)
        sin_table = sin_f.astype(jnp.bfloat16)
        cos_table, sin_table = lax.optimization_barrier((cos_table, sin_table))
        tensor_product = (((1,), (1,)), ((), ()))
        s_cos = lax.dot_general(
            charge_live, cos_table, tensor_product, preferred_element_type=jnp.float32
        )
        s_sin = lax.dot_general(
            charge_live, sin_table, tensor_product, preferred_element_type=jnp.float32
        )
        s_both = butterfly_sum(jnp.stack([s_cos, s_sin], 0), "dom", n_dom)
        cos_side, sin_side = reciprocal_filter_weight(
            s_both[0], s_both[1], cartesian_mode_vector, gaussian_spread, atoms_total
        )
        field = jnp.dot(cos_side, cos_table, preferred_element_type=jnp.float32)
        field = field + jnp.dot(sin_side, sin_table, preferred_element_type=jnp.float32)
        charge_f = charge_live.astype(jnp.float32)
        head = jnp.where(live[None, :], field[:channels], 0.0)
        force_rows = [
            jnp.sum(charge_f * field[channels * (1 + d) : channels * (2 + d)], 0, keepdims=True)
            for d in range(3)
        ]
        partial = jnp.concatenate([head] + force_rows, 0)
        rows = n_local // n_ka
        blocks = jnp.stack([partial[:, b * rows : (b + 1) * rows] for b in range(n_ka)], 0)
        own = halving_scatter(blocks, "ka", n_ka)
        return (own[:channels], own[channels:])

    return local


def solution(mesh):
    placed = (P(None, "dom"), P(None, "dom"), P(None, "ka"), P("dom"), P())
    return jax.shard_map(
        make_local(mesh.shape["dom"], mesh.shape["ka"]),
        mesh=mesh,
        in_specs=placed,
        out_specs=(P(None, ("dom", "ka")), P(None, ("dom", "ka"))),
        check_vma=False,
    )
```

```python
import math

import jax
import jax.numpy as jnp
from jax import lax
from jax.experimental import pallas as pl
from jax.sharding import PartitionSpec as P

two_pi = 6.283185307179586
box_length = 125.0

_SIN_C = [3.1415926399240375, -5.167710053300693, 2.5500768575243145, -0.5982866957251158,
          0.0776479208030991]
_COS_C = [0.9999999525693762, -4.934792730768449, 4.058409142115622, -1.3318612751935888,
          0.2196570817648336]
_ROOT2 = math.sqrt(2.0)


def turns_cos_sin(t):
    r = t - jnp.floor(t + 0.5)
    r2 = r * r
    s = jnp.float32(_SIN_C[-1] * _ROOT2)
    for coef in _SIN_C[-2::-1]:
        s = s * r2 + jnp.float32(coef * _ROOT2)
    s = s * r
    c = jnp.float32(_COS_C[-1] * _ROOT2)
    for coef in _COS_C[-2::-1]:
        c = c * r2 + jnp.float32(coef * _ROOT2)
    cos_out = 1.0 - s * s
    sin_out = s * c
    return cos_out, sin_out


def field_kernel(cs_ref, ss_ref, ct_ref, st_ref, q_ref, live_ref, out_ref):
    field = jnp.dot(cs_ref[...], ct_ref[...], preferred_element_type=jnp.float32)
    field = field + jnp.dot(ss_ref[...], st_ref[...], preferred_element_type=jnp.float32)
    channels = q_ref.shape[0]
    live = live_ref[...] > 0.0
    out_ref[0, :channels, :] = jnp.where(live, field[:channels], 0.0)
    q = q_ref[...].astype(jnp.float32)
    for d in range(3):
        rows = field[channels * (1 + d) : channels * (2 + d)]
        out_ref[0, channels + d : channels + d + 1, :] = jnp.sum(q * rows, 0, keepdims=True)


def field_blocks(cos_side, sin_side, cos_table, sin_table, charge_live, live_f, n_blocks):
    n_side, n_k = cos_side.shape
    channels, n_at = charge_live.shape
    rows = n_at // n_blocks
    return pl.pallas_call(
        field_kernel,
        grid=(n_blocks,),
        in_specs=[
            pl.BlockSpec((n_side, n_k), lambda b: (0, 0)),
            pl.BlockSpec((n_side, n_k), lambda b: (0, 0)),
            pl.BlockSpec((n_k, rows), lambda b: (0, b)),
            pl.BlockSpec((n_k, rows), lambda b: (0, b)),
            pl.BlockSpec((channels, rows), lambda b: (0, b)),
            pl.BlockSpec((1, rows), lambda b: (0, b)),
        ],
        out_specs=pl.BlockSpec((1, channels + 3, rows), lambda b: (b, 0, 0)),
        out_shape=jax.ShapeDtypeStruct((n_blocks, channels + 3, rows), jnp.float32),
    )(cos_side, sin_side, cos_table, sin_table, charge_live, live_f)


def reciprocal_filter_weight(s_cos, s_sin, cartesian_mode_vector, gaussian_spread, atoms_total):
    norm_sq = (
        cartesian_mode_vector[0] * cartesian_mode_vector[0]
        + cartesian_mode_vector[1] * cartesian_mode_vector[1]
        + cartesian_mode_vector[2] * cartesian_mode_vector[2]
    )
    scale = two_pi / box_length
    wavevector_norm_squared = scale * scale * norm_sq
    kernel = (
        2.0
        * jnp.exp(
            -0.5 * (gaussian_spread * gaussian_spread)[:, None] * wavevector_norm_squared[None, :]
        )
        / norm_sq[None, :]
        / jnp.sqrt(jnp.float32(atoms_total))
    )
    partial_first_term = kernel * s_cos
    partial_second_term = kernel * s_sin
    cos_side = jnp.concatenate(
        [
            partial_first_term,
            -scale * cartesian_mode_vector[0] * partial_second_term,
            -scale * cartesian_mode_vector[1] * partial_second_term,
            -scale * cartesian_mode_vector[2] * partial_second_term,
        ],
        0,
    )
    sin_side = jnp.concatenate(
        [
            partial_second_term,
            scale * cartesian_mode_vector[0] * partial_first_term,
            scale * cartesian_mode_vector[1] * partial_first_term,
            scale * cartesian_mode_vector[2] * partial_first_term,
        ],
        0,
    )
    return (cos_side.astype(jnp.bfloat16), sin_side.astype(jnp.bfloat16))


def butterfly_sum(x, axis, n):
    step = 1
    while step < n:
        x = x + lax.ppermute(x, axis, [(i, i ^ step) for i in range(n)])
        step *= 2
    return x


def halving_scatter(held, axis, n):
    me = lax.axis_index(axis)
    step = 1
    while step < n:
        m = held.shape[0]
        pairs = held.reshape(m // 2, 2, *held.shape[1:])
        bit = (me // step) % 2
        keep = jnp.where(bit == 0, pairs[:, 0], pairs[:, 1])
        send = jnp.where(bit == 0, pairs[:, 1], pairs[:, 0])
        pairs_list = [(i, i ^ step) for i in range(n)]
        if step >= 2:
            recv = lax.ppermute(send.astype(jnp.bfloat16), axis, pairs_list).astype(jnp.float32)
        else:
            recv = lax.ppermute(send, axis, pairs_list)
        held = keep + recv
        step *= 2
    return held[0]


def make_local(n_dom, n_ka):
    def local(
        cell_coordinates_frac, site_strengths, miller_indices, occupied_site_tally, gaussian_spread
    ):
        channels = site_strengths.shape[0]
        n_local = cell_coordinates_frac.shape[1]
        atoms_total = n_local * n_dom
        live = jnp.arange(n_local) < occupied_site_tally[0]
        charge_live = jnp.where(live[None, :], site_strengths, jnp.zeros_like(site_strengths))
        cartesian_mode_vector = miller_indices.astype(jnp.float32)
        t = (
            cartesian_mode_vector[0][:, None] * cell_coordinates_frac[0][None, :]
            + cartesian_mode_vector[1][:, None] * cell_coordinates_frac[1][None, :]
            + cartesian_mode_vector[2][:, None] * cell_coordinates_frac[2][None, :]
        )
        cos_f, sin_f = turns_cos_sin(t)
        cos_table = cos_f.astype(jnp.bfloat16)
        sin_table = sin_f.astype(jnp.bfloat16)
        cos_table, sin_table = lax.optimization_barrier((cos_table, sin_table))
        tensor_product = (((1,), (1,)), ((), ()))
        s_cos = lax.dot_general(
            charge_live, cos_table, tensor_product, preferred_element_type=jnp.float32
        )
        s_sin = lax.dot_general(
            charge_live, sin_table, tensor_product, preferred_element_type=jnp.float32
        )
        s_both = butterfly_sum(jnp.stack([s_cos, s_sin], 0), "dom", n_dom)
        cos_side, sin_side = reciprocal_filter_weight(
            s_both[0], s_both[1], cartesian_mode_vector, gaussian_spread, atoms_total
        )
        blocks = field_blocks(
            cos_side, sin_side, cos_table, sin_table, charge_live,
            live.astype(jnp.float32)[None, :], n_ka,
        )
        own = halving_scatter(blocks, "ka", n_ka)
        return (own[:channels], own[channels:])

    return local


def solution(mesh):
    placed = (P(None, "dom"), P(None, "dom"), P(None, "ka"), P("dom"), P())
    return jax.shard_map(
        make_local(mesh.shape["dom"], mesh.shape["ka"]),
        mesh=mesh,
        in_specs=placed,
        out_specs=(P(None, ("dom", "ka")), P(None, ("dom", "ka"))),
        check_vma=False,
    )
```

```python
import math

import jax
import jax.numpy as jnp
from jax import lax
from jax.sharding import PartitionSpec as P

two_pi = 6.283185307179586
box_length = 125.0

_SIN_C = [3.1415926399240375, -5.167710053300693, 2.5500768575243145, -0.5982866957251158,
          0.0776479208030991]
_COS_C = [0.9999999525693762, -4.934792730768449, 4.058409142115622, -1.3318612751935888,
          0.2196570817648336]
_ROOT2 = math.sqrt(2.0)


def turns_cos_sin(t):
    r = t - jnp.floor(t + 0.5)
    r2 = r * r
    s = jnp.float32(_SIN_C[-1] * _ROOT2)
    for coef in _SIN_C[-2::-1]:
        s = s * r2 + jnp.float32(coef * _ROOT2)
    s = s * r
    c = jnp.float32(_COS_C[-1] * _ROOT2)
    for coef in _COS_C[-2::-1]:
        c = c * r2 + jnp.float32(coef * _ROOT2)
    cos_out = 1.0 - s * s
    sin_out = s * c
    return cos_out, sin_out


def reciprocal_filter_weight(s_cos, s_sin, cartesian_mode_vector, gaussian_spread, atoms_total):
    norm_sq = (
        cartesian_mode_vector[0] * cartesian_mode_vector[0]
        + cartesian_mode_vector[1] * cartesian_mode_vector[1]
        + cartesian_mode_vector[2] * cartesian_mode_vector[2]
    )
    scale = two_pi / box_length
    wavevector_norm_squared = scale * scale * norm_sq
    kernel = (
        2.0
        * jnp.exp(
            -0.5 * (gaussian_spread * gaussian_spread)[:, None] * wavevector_norm_squared[None, :]
        )
        / norm_sq[None, :]
        / jnp.sqrt(jnp.float32(atoms_total))
    )
    partial_first_term = kernel * s_cos
    partial_second_term = kernel * s_sin
    cos_side = jnp.concatenate(
        [
            partial_first_term,
            -scale * cartesian_mode_vector[0] * partial_second_term,
            -scale * cartesian_mode_vector[1] * partial_second_term,
            -scale * cartesian_mode_vector[2] * partial_second_term,
        ],
        0,
    )
    sin_side = jnp.concatenate(
        [
            partial_second_term,
            scale * cartesian_mode_vector[0] * partial_first_term,
            scale * cartesian_mode_vector[1] * partial_first_term,
            scale * cartesian_mode_vector[2] * partial_first_term,
        ],
        0,
    )
    return (cos_side.astype(jnp.bfloat16), sin_side.astype(jnp.bfloat16))


def butterfly_sum(x, axis, n):
    step = 1
    while step < n:
        x = x + lax.ppermute(x, axis, [(i, i ^ step) for i in range(n)])
        step *= 2
    return x


def halving_scatter(held, axis, n):
    me = lax.axis_index(axis)
    step = 1
    while step < n:
        m = held.shape[0]
        pairs = held.reshape(m // 2, 2, *held.shape[1:])
        bit = (me // step) % 2
        keep = jnp.where(bit == 0, pairs[:, 0], pairs[:, 1])
        send = jnp.where(bit == 0, pairs[:, 1], pairs[:, 0])
        pairs_list = [(i, i ^ step) for i in range(n)]
        if step >= 2:
            recv = lax.ppermute(send.astype(jnp.bfloat16), axis, pairs_list).astype(jnp.float32)
        else:
            recv = lax.ppermute(send, axis, pairs_list)
        held = keep + recv
        step *= 2
    return held[0]


def make_local(n_dom, n_ka):
    def local(
        cell_coordinates_frac, site_strengths, miller_indices, occupied_site_tally, gaussian_spread
    ):
        channels = site_strengths.shape[0]
        n_local = cell_coordinates_frac.shape[1]
        atoms_total = n_local * n_dom
        live = jnp.arange(n_local) < occupied_site_tally[0]
        charge_live = jnp.where(live[None, :], site_strengths, jnp.zeros_like(site_strengths))
        cartesian_mode_vector = miller_indices.astype(jnp.float32)
        t = (
            cartesian_mode_vector[0][:, None] * cell_coordinates_frac[0][None, :]
            + cartesian_mode_vector[1][:, None] * cell_coordinates_frac[1][None, :]
            + cartesian_mode_vector[2][:, None] * cell_coordinates_frac[2][None, :]
        )
        cos_f, sin_f = turns_cos_sin(t)
        cos_table = cos_f.astype(jnp.bfloat16)
        sin_table = sin_f.astype(jnp.bfloat16)
        cos_table, sin_table = lax.optimization_barrier((cos_table, sin_table))
        tensor_product = (((1,), (1,)), ((), ()))
        s_cos = lax.dot_general(
            charge_live, cos_table, tensor_product, preferred_element_type=jnp.float32
        )
        s_sin = lax.dot_general(
            charge_live, sin_table, tensor_product, preferred_element_type=jnp.float32
        )
        s_both = butterfly_sum(jnp.stack([s_cos, s_sin], 0), "dom", n_dom)
        cos_side, sin_side = reciprocal_filter_weight(
            s_both[0], s_both[1], cartesian_mode_vector, gaussian_spread, atoms_total
        )
        field = lax.dot_general(
            jnp.stack([cos_side, sin_side], 0), jnp.stack([cos_table, sin_table], 0),
            (((0, 2), (0, 1)), ((), ())), preferred_element_type=jnp.float32,
        )
        charge_f = charge_live.astype(jnp.float32)
        head = jnp.where(live[None, :], field[:channels], 0.0)
        force_rows = [
            jnp.sum(charge_f * field[channels * (1 + d) : channels * (2 + d)], 0, keepdims=True)
            for d in range(3)
        ]
        partial = jnp.concatenate([head] + force_rows, 0)
        rows = n_local // n_ka
        blocks = jnp.stack([partial[:, b * rows : (b + 1) * rows] for b in range(n_ka)], 0)
        own = halving_scatter(blocks, "ka", n_ka)
        return (own[:channels], own[channels:])

    return local


def solution(mesh):
    placed = (P(None, "dom"), P(None, "dom"), P(None, "ka"), P("dom"), P())
    return jax.shard_map(
        make_local(mesh.shape["dom"], mesh.shape["ka"]),
        mesh=mesh,
        in_specs=placed,
        out_specs=(P(None, ("dom", "ka")), P(None, ("dom", "ka"))),
        check_vma=False,
    )
```

```python
import math

import jax
import jax.numpy as jnp
from jax import lax
from jax.sharding import PartitionSpec as P

two_pi = 6.283185307179586
box_length = 125.0

_SIN_C = [3.1415926399240375, -5.167710053300693, 2.5500768575243145, -0.5982866957251158,
          0.0776479208030991]
_COS_C = [0.9999999525693762, -4.934792730768449, 4.058409142115622, -1.3318612751935888,
          0.2196570817648336]
_ROOT2 = math.sqrt(2.0)


def turns_cos_sin(t):
    r = t - jnp.floor(t + 0.5)
    r2 = r * r
    s = jnp.float32(_SIN_C[-1] * _ROOT2)
    for coef in _SIN_C[-2::-1]:
        s = s * r2 + jnp.float32(coef * _ROOT2)
    s = s * r
    c = jnp.float32(_COS_C[-1] * _ROOT2)
    for coef in _COS_C[-2::-1]:
        c = c * r2 + jnp.float32(coef * _ROOT2)
    cos_out = 1.0 - s * s
    sin_out = s * c
    return cos_out, sin_out


def reciprocal_filter_weight(s_cos, s_sin, cartesian_mode_vector, gaussian_spread, atoms_total):
    norm_sq = (
        cartesian_mode_vector[0] * cartesian_mode_vector[0]
        + cartesian_mode_vector[1] * cartesian_mode_vector[1]
        + cartesian_mode_vector[2] * cartesian_mode_vector[2]
    )
    scale = two_pi / box_length
    wavevector_norm_squared = scale * scale * norm_sq
    kernel = (
        2.0
        * jnp.exp(
            -0.5 * (gaussian_spread * gaussian_spread)[:, None] * wavevector_norm_squared[None, :]
        )
        / norm_sq[None, :]
        / jnp.sqrt(jnp.float32(atoms_total))
    )
    partial_first_term = kernel * s_cos
    partial_second_term = kernel * s_sin
    cos_side = jnp.concatenate(
        [
            partial_first_term,
            -scale * cartesian_mode_vector[0] * partial_second_term,
            -scale * cartesian_mode_vector[1] * partial_second_term,
            -scale * cartesian_mode_vector[2] * partial_second_term,
        ],
        0,
    )
    sin_side = jnp.concatenate(
        [
            partial_second_term,
            scale * cartesian_mode_vector[0] * partial_first_term,
            scale * cartesian_mode_vector[1] * partial_first_term,
            scale * cartesian_mode_vector[2] * partial_first_term,
        ],
        0,
    )
    return (cos_side.astype(jnp.bfloat16), sin_side.astype(jnp.bfloat16))


def butterfly_sum(x, axis, n):
    step = 1
    while step < n:
        x = x + lax.ppermute(x, axis, [(i, i ^ step) for i in range(n)])
        step *= 2
    return x


def halving_rest(held, axis, n, step):
    me = lax.axis_index(axis)
    while step < n:
        m = held.shape[0]
        pairs = held.reshape(m // 2, 2, *held.shape[1:])
        bit = (me // step) % 2
        keep = jnp.where(bit == 0, pairs[:, 0], pairs[:, 1])
        send = jnp.where(bit == 0, pairs[:, 1], pairs[:, 0])
        pairs_list = [(i, i ^ step) for i in range(n)]
        if step >= 2:
            recv = lax.ppermute(send.astype(jnp.bfloat16), axis, pairs_list).astype(jnp.float32)
        else:
            recv = lax.ppermute(send, axis, pairs_list)
        held = keep + recv
        step *= 2
    return held[0]


def make_local(n_dom, n_ka):
    def local(
        cell_coordinates_frac, site_strengths, miller_indices, occupied_site_tally, gaussian_spread
    ):
        channels = site_strengths.shape[0]
        n_local = cell_coordinates_frac.shape[1]
        atoms_total = n_local * n_dom
        rows = n_local // n_ka
        bit0 = lax.axis_index("ka") % 2
        odd_first = [b for b in range(1, n_ka, 2)] + [b for b in range(0, n_ka, 2)]
        even_first = [b for b in range(0, n_ka, 2)] + [b for b in range(1, n_ka, 2)]

        def ordered(x):
            x4 = x.reshape(x.shape[0], n_ka, rows)
            return jnp.where(bit0 == 0, x4[:, odd_first], x4[:, even_first]).reshape(x.shape)

        slots = ordered(jnp.arange(n_local, dtype=jnp.int32)[None, :])[0]
        live = slots < occupied_site_tally[0]
        pos = ordered(cell_coordinates_frac)
        charge_live = jnp.where(live[None, :], ordered(site_strengths), jnp.zeros_like(site_strengths))
        cartesian_mode_vector = miller_indices.astype(jnp.float32)
        t = (
            cartesian_mode_vector[0][:, None] * pos[0][None, :]
            + cartesian_mode_vector[1][:, None] * pos[1][None, :]
            + cartesian_mode_vector[2][:, None] * pos[2][None, :]
        )
        cos_f, sin_f = turns_cos_sin(t)
        cos_table = cos_f.astype(jnp.bfloat16)
        sin_table = sin_f.astype(jnp.bfloat16)
        cos_table, sin_table = lax.optimization_barrier((cos_table, sin_table))
        tensor_product = (((1,), (1,)), ((), ()))
        s_cos = lax.dot_general(
            charge_live, cos_table, tensor_product, preferred_element_type=jnp.float32
        )
        s_sin = lax.dot_general(
            charge_live, sin_table, tensor_product, preferred_element_type=jnp.float32
        )
        s_both = butterfly_sum(jnp.stack([s_cos, s_sin], 0), "dom", n_dom)
        cos_side, sin_side = reciprocal_filter_weight(
            s_both[0], s_both[1], cartesian_mode_vector, gaussian_spread, atoms_total
        )
        charge_f = charge_live.astype(jnp.float32)
        half = n_local // 2

        def partial_blocks(lo):
            cols = slice(lo, lo + half)
            field = jnp.dot(cos_side, cos_table[:, cols], preferred_element_type=jnp.float32)
            field = field + jnp.dot(sin_side, sin_table[:, cols], preferred_element_type=jnp.float32)
            head = jnp.where(live[None, cols], field[:channels], 0.0)
            force_rows = [
                jnp.sum(charge_f[:, cols] * field[channels * (1 + d) : channels * (2 + d)], 0, keepdims=True)
                for d in range(3)
            ]
            partial = jnp.concatenate([head] + force_rows, 0)
            return jnp.stack([partial[:, j * rows : (j + 1) * rows] for j in range(n_ka // 2)], 0)

        sent = partial_blocks(0)
        sent, cos_side, sin_side = lax.optimization_barrier((sent, cos_side, sin_side))
        recv = lax.ppermute(sent, "ka", [(i, i ^ 1) for i in range(n_ka)])
        held = partial_blocks(half) + recv
        own = halving_rest(held, "ka", n_ka, 2)
        return (own[:channels], own[channels:])

    return local


def solution(mesh):
    placed = (P(None, "dom"), P(None, "dom"), P(None, "ka"), P("dom"), P())
    return jax.shard_map(
        make_local(mesh.shape["dom"], mesh.shape["ka"]),
        mesh=mesh,
        in_specs=placed,
        out_specs=(P(None, ("dom", "ka")), P(None, ("dom", "ka"))),
        check_vma=False,
    )
```

```python
import math

import jax
import jax.numpy as jnp
from jax import lax
from jax.sharding import PartitionSpec as P

two_pi = 6.283185307179586
box_length = 125.0

_SIN_C = [3.1415926399240375, -5.167710053300693, 2.5500768575243145, -0.5982866957251158,
          0.0776479208030991]
_COS_C = [0.9999999525693762, -4.934792730768449, 4.058409142115622, -1.3318612751935888,
          0.2196570817648336]
_ROOT2 = math.sqrt(2.0)


def turns_cos_sin(t):
    r = t - jnp.floor(t + 0.5)
    r2 = r * r
    s = jnp.float32(_SIN_C[-1] * _ROOT2)
    for coef in _SIN_C[-2::-1]:
        s = s * r2 + jnp.float32(coef * _ROOT2)
    s = s * r
    c = jnp.float32(_COS_C[-1] * _ROOT2)
    for coef in _COS_C[-2::-1]:
        c = c * r2 + jnp.float32(coef * _ROOT2)
    cos_out = 1.0 - s * s
    sin_out = s * c
    return cos_out, sin_out


def reciprocal_filter_weight(s_cos, s_sin, cartesian_mode_vector, gaussian_spread, atoms_total):
    norm_sq = (
        cartesian_mode_vector[0] * cartesian_mode_vector[0]
        + cartesian_mode_vector[1] * cartesian_mode_vector[1]
        + cartesian_mode_vector[2] * cartesian_mode_vector[2]
    )
    scale = two_pi / box_length
    wavevector_norm_squared = scale * scale * norm_sq
    kernel = (
        2.0
        * jnp.exp(
            -0.5 * (gaussian_spread * gaussian_spread)[:, None] * wavevector_norm_squared[None, :]
        )
        / norm_sq[None, :]
        / jnp.sqrt(jnp.float32(atoms_total))
    )
    partial_first_term = kernel * s_cos
    partial_second_term = kernel * s_sin
    cos_side = jnp.concatenate(
        [
            partial_first_term,
            -scale * cartesian_mode_vector[0] * partial_second_term,
            -scale * cartesian_mode_vector[1] * partial_second_term,
            -scale * cartesian_mode_vector[2] * partial_second_term,
        ],
        0,
    )
    sin_side = jnp.concatenate(
        [
            partial_second_term,
            scale * cartesian_mode_vector[0] * partial_first_term,
            scale * cartesian_mode_vector[1] * partial_first_term,
            scale * cartesian_mode_vector[2] * partial_first_term,
        ],
        0,
    )
    return (cos_side.astype(jnp.bfloat16), sin_side.astype(jnp.bfloat16))


def butterfly_sum(x, axis, n):
    step = 1
    while step < n:
        x = x + lax.ppermute(x, axis, [(i, i ^ step) for i in range(n)])
        step *= 2
    return x


def halving_scatter(held, axis, n):
    me = lax.axis_index(axis)
    step = 1
    while step < n:
        m = held.shape[0]
        pairs = held.reshape(m // 2, 2, *held.shape[1:])
        bit = (me // step) % 2
        keep = jnp.where(bit == 0, pairs[:, 0], pairs[:, 1])
        send = jnp.where(bit == 0, pairs[:, 1], pairs[:, 0])
        pairs_list = [(i, i ^ step) for i in range(n)]
        if step >= 2:
            recv = lax.ppermute(send.astype(jnp.bfloat16), axis, pairs_list)
        else:
            recv = lax.ppermute(send, axis, pairs_list)
        if step * 2 >= n:
            return keep[0], recv[0]
        recv = recv.astype(jnp.float32)
        held = keep + recv
        step *= 2
    return held[0], jnp.zeros_like(held[0])


def make_local(n_dom, n_ka):
    def local(
        cell_coordinates_frac, site_strengths, miller_indices, occupied_site_tally, gaussian_spread
    ):
        channels = site_strengths.shape[0]
        n_local = cell_coordinates_frac.shape[1]
        atoms_total = n_local * n_dom
        live = jnp.arange(n_local) < occupied_site_tally[0]
        charge_live = jnp.where(live[None, :], site_strengths, jnp.zeros_like(site_strengths))
        cartesian_mode_vector = miller_indices.astype(jnp.float32)
        t = (
            cartesian_mode_vector[0][:, None] * cell_coordinates_frac[0][None, :]
            + cartesian_mode_vector[1][:, None] * cell_coordinates_frac[1][None, :]
            + cartesian_mode_vector[2][:, None] * cell_coordinates_frac[2][None, :]
        )
        cos_f, sin_f = turns_cos_sin(t)
        cos_table = cos_f.astype(jnp.bfloat16)
        sin_table = sin_f.astype(jnp.bfloat16)
        cos_table, sin_table = lax.optimization_barrier((cos_table, sin_table))
        tensor_product = (((1,), (1,)), ((), ()))
        s_cos = lax.dot_general(
            charge_live, cos_table, tensor_product, preferred_element_type=jnp.float32
        )
        s_sin = lax.dot_general(
            charge_live, sin_table, tensor_product, preferred_element_type=jnp.float32
        )
        s_both = butterfly_sum(jnp.stack([s_cos, s_sin], 0), "dom", n_dom)
        cos_side, sin_side = reciprocal_filter_weight(
            s_both[0], s_both[1], cartesian_mode_vector, gaussian_spread, atoms_total
        )
        field = jnp.dot(cos_side, cos_table, preferred_element_type=jnp.float32)
        field = field + jnp.dot(sin_side, sin_table, preferred_element_type=jnp.float32)
        charge_f = charge_live.astype(jnp.float32)
        head = jnp.where(live[None, :], field[:channels], 0.0)
        force_rows = [
            jnp.sum(charge_f * field[channels * (1 + d) : channels * (2 + d)], 0, keepdims=True)
            for d in range(3)
        ]
        partial = jnp.concatenate([head] + force_rows, 0)
        rows = n_local // n_ka
        blocks = jnp.stack([partial[:, b * rows : (b + 1) * rows] for b in range(n_ka)], 0)
        own, other = halving_scatter(blocks, "ka", n_ka)
        potential = own[:channels] + other[:channels].astype(jnp.float32)
        forces = own[channels:] + other[channels:].astype(jnp.float32)
        return (potential, forces)

    return local


def solution(mesh):
    placed = (P(None, "dom"), P(None, "dom"), P(None, "ka"), P("dom"), P())
    return jax.shard_map(
        make_local(mesh.shape["dom"], mesh.shape["ka"]),
        mesh=mesh,
        in_specs=placed,
        out_specs=(P(None, ("dom", "ka")), P(None, ("dom", "ka"))),
        check_vma=False,
    )
```

```python
import math

import jax
import jax.numpy as jnp
from jax import lax
from jax.sharding import PartitionSpec as P

two_pi = 6.283185307179586
box_length = 125.0

_SIN_C = [3.1415926399240375, -5.167710053300693, 2.5500768575243145, -0.5982866957251158,
          0.0776479208030991]
_COS_C = [0.9999999525693762, -4.934792730768449, 4.058409142115622, -1.3318612751935888,
          0.2196570817648336]
_ROOT2 = math.sqrt(2.0)


def turns_cos_sin(t):
    r = t - jnp.floor(t + 0.5)
    r2 = r * r
    s = jnp.float32(_SIN_C[-1] * _ROOT2)
    for coef in _SIN_C[-2::-1]:
        s = s * r2 + jnp.float32(coef * _ROOT2)
    s = s * r
    c = jnp.float32(_COS_C[-1] * _ROOT2)
    for coef in _COS_C[-2::-1]:
        c = c * r2 + jnp.float32(coef * _ROOT2)
    cos_out = 1.0 - s * s
    sin_out = s * c
    return cos_out, sin_out


def reciprocal_filter_weight(s_cos, s_sin, cartesian_mode_vector, gaussian_spread, atoms_total):
    norm_sq = (
        cartesian_mode_vector[0] * cartesian_mode_vector[0]
        + cartesian_mode_vector[1] * cartesian_mode_vector[1]
        + cartesian_mode_vector[2] * cartesian_mode_vector[2]
    )
    scale = two_pi / box_length
    wavevector_norm_squared = scale * scale * norm_sq
    kernel = (
        2.0
        * jnp.exp(
            -0.5 * (gaussian_spread * gaussian_spread)[:, None] * wavevector_norm_squared[None, :]
        )
        / norm_sq[None, :]
        / jnp.sqrt(jnp.float32(atoms_total))
    )
    partial_first_term = kernel * s_cos
    partial_second_term = kernel * s_sin
    cos_side = jnp.concatenate(
        [
            partial_first_term,
            -scale * cartesian_mode_vector[0] * partial_second_term,
            -scale * cartesian_mode_vector[1] * partial_second_term,
            -scale * cartesian_mode_vector[2] * partial_second_term,
        ],
        0,
    )
    sin_side = jnp.concatenate(
        [
            partial_second_term,
            scale * cartesian_mode_vector[0] * partial_first_term,
            scale * cartesian_mode_vector[1] * partial_first_term,
            scale * cartesian_mode_vector[2] * partial_first_term,
        ],
        0,
    )
    return (cos_side.astype(jnp.bfloat16), sin_side.astype(jnp.bfloat16))


def butterfly_sum(x, n_dom, n_ka):
    bits = []
    step = 1
    while step < n_dom:
        bits.append(step)
        step *= 2
    turn = (len(bits) + 1) // 2
    orders = (bits, bits[turn:] + bits[:turn])
    for j in range(len(bits)):
        pairs = []
        for i in range(n_dom * n_ka):
            d, a = divmod(i, n_ka)
            pairs.append((i, (d ^ orders[a % 2][j]) * n_ka + a))
        x = x + lax.ppermute(x, ("dom", "ka"), pairs)
    return x


def halving_scatter(held, axis, n):
    me = lax.axis_index(axis)
    step = 1
    while step < n:
        m = held.shape[0]
        pairs = held.reshape(m // 2, 2, *held.shape[1:])
        bit = (me // step) % 2
        keep = jnp.where(bit == 0, pairs[:, 0], pairs[:, 1])
        send = jnp.where(bit == 0, pairs[:, 1], pairs[:, 0])
        pairs_list = [(i, i ^ step) for i in range(n)]
        if step >= 2:
            recv = lax.ppermute(send.astype(jnp.bfloat16), axis, pairs_list)
        else:
            recv = lax.ppermute(send, axis, pairs_list)
        if step * 2 >= n:
            return keep[0], recv[0]
        recv = recv.astype(jnp.float32)
        held = keep + recv
        step *= 2
    return held[0], jnp.zeros_like(held[0])


def make_local(n_dom, n_ka):
    def local(
        cell_coordinates_frac, site_strengths, miller_indices, occupied_site_tally, gaussian_spread
    ):
        channels = site_strengths.shape[0]
        n_local = cell_coordinates_frac.shape[1]
        atoms_total = n_local * n_dom
        live = jnp.arange(n_local) < occupied_site_tally[0]
        charge_live = jnp.where(live[None, :], site_strengths, jnp.zeros_like(site_strengths))
        cartesian_mode_vector = miller_indices.astype(jnp.float32)
        t = (
            cartesian_mode_vector[0][:, None] * cell_coordinates_frac[0][None, :]
            + cartesian_mode_vector[1][:, None] * cell_coordinates_frac[1][None, :]
            + cartesian_mode_vector[2][:, None] * cell_coordinates_frac[2][None, :]
        )
        cos_f, sin_f = turns_cos_sin(t)
        cos_table = cos_f.astype(jnp.bfloat16)
        sin_table = sin_f.astype(jnp.bfloat16)
        cos_table, sin_table = lax.optimization_barrier((cos_table, sin_table))
        tensor_product = (((1,), (1,)), ((), ()))
        s_cos = lax.dot_general(
            charge_live, cos_table, tensor_product, preferred_element_type=jnp.float32
        )
        s_sin = lax.dot_general(
            charge_live, sin_table, tensor_product, preferred_element_type=jnp.float32
        )
        s_both = butterfly_sum(jnp.stack([s_cos, s_sin], 0), n_dom, n_ka)
        cos_side, sin_side = reciprocal_filter_weight(
            s_both[0], s_both[1], cartesian_mode_vector, gaussian_spread, atoms_total
        )
        field = jnp.dot(cos_side, cos_table, preferred_element_type=jnp.float32)
        field = field + jnp.dot(sin_side, sin_table, preferred_element_type=jnp.float32)
        charge_f = charge_live.astype(jnp.float32)
        head = jnp.where(live[None, :], field[:channels], 0.0)
        force_rows = [
            jnp.sum(charge_f * field[channels * (1 + d) : channels * (2 + d)], 0, keepdims=True)
            for d in range(3)
        ]
        partial = jnp.concatenate([head] + force_rows, 0)
        rows = n_local // n_ka
        blocks = jnp.stack([partial[:, b * rows : (b + 1) * rows] for b in range(n_ka)], 0)
        own, other = halving_scatter(blocks, "ka", n_ka)
        potential = own[:channels] + other[:channels].astype(jnp.float32)
        forces = own[channels:] + other[channels:].astype(jnp.float32)
        return (potential, forces)

    return local


def solution(mesh):
    placed = (P(None, "dom"), P(None, "dom"), P(None, "ka"), P("dom"), P())
    return jax.shard_map(
        make_local(mesh.shape["dom"], mesh.shape["ka"]),
        mesh=mesh,
        in_specs=placed,
        out_specs=(P(None, ("dom", "ka")), P(None, ("dom", "ka"))),
        check_vma=False,
    )
```

```python
import math

import jax
import jax.numpy as jnp
from jax import lax
from jax.sharding import PartitionSpec as P

two_pi = 6.283185307179586
box_length = 125.0

_SIN_C = [3.1415926399240375, -5.167710053300693, 2.5500768575243145, -0.5982866957251158,
          0.0776479208030991]
_COS_C = [0.9999999525693762, -4.934792730768449, 4.058409142115622, -1.3318612751935888,
          0.2196570817648336]
_ROOT2 = math.sqrt(2.0)


def turns_cos_sin(t):
    r = t - lax.round(t, lax.RoundingMethod.TO_NEAREST_EVEN)
    r2 = r * r
    s = jnp.float32(_SIN_C[-1] * _ROOT2)
    for coef in _SIN_C[-2::-1]:
        s = s * r2 + jnp.float32(coef * _ROOT2)
    s = s * r
    c = jnp.float32(_COS_C[-1] * _ROOT2)
    for coef in _COS_C[-2::-1]:
        c = c * r2 + jnp.float32(coef * _ROOT2)
    cos_out = 1.0 - s * s
    sin_out = s * c
    return cos_out, sin_out


def reciprocal_filter_weight(s_cos, s_sin, cartesian_mode_vector, gaussian_spread, atoms_total):
    norm_sq = (
        cartesian_mode_vector[0] * cartesian_mode_vector[0]
        + cartesian_mode_vector[1] * cartesian_mode_vector[1]
        + cartesian_mode_vector[2] * cartesian_mode_vector[2]
    )
    scale = two_pi / box_length
    wavevector_norm_squared = scale * scale * norm_sq
    kernel = (
        2.0
        * jnp.exp(
            -0.5 * (gaussian_spread * gaussian_spread)[:, None] * wavevector_norm_squared[None, :]
        )
        / norm_sq[None, :]
        / jnp.sqrt(jnp.float32(atoms_total))
    )
    partial_first_term = kernel * s_cos
    partial_second_term = kernel * s_sin
    cos_side = jnp.concatenate(
        [
            partial_first_term,
            -scale * cartesian_mode_vector[0] * partial_second_term,
            -scale * cartesian_mode_vector[1] * partial_second_term,
            -scale * cartesian_mode_vector[2] * partial_second_term,
        ],
        0,
    )
    sin_side = jnp.concatenate(
        [
            partial_second_term,
            scale * cartesian_mode_vector[0] * partial_first_term,
            scale * cartesian_mode_vector[1] * partial_first_term,
            scale * cartesian_mode_vector[2] * partial_first_term,
        ],
        0,
    )
    return (cos_side.astype(jnp.bfloat16), sin_side.astype(jnp.bfloat16))


def butterfly_sum(x, n_dom, n_ka):
    bits = []
    step = 1
    while step < n_dom:
        bits.append(step)
        step *= 2
    turn = (len(bits) + 1) // 2
    orders = (bits, bits[turn:] + bits[:turn])
    for j in range(len(bits)):
        pairs = []
        for i in range(n_dom * n_ka):
            d, a = divmod(i, n_ka)
            pairs.append((i, (d ^ orders[a % 2][j]) * n_ka + a))
        x = x + lax.ppermute(x, ("dom", "ka"), pairs)
    return x


def halving_scatter(held, axis, n):
    me = lax.axis_index(axis)
    step = 1
    while step < n:
        m = held.shape[0]
        pairs = held.reshape(m // 2, 2, *held.shape[1:])
        bit = (me // step) % 2
        keep = jnp.where(bit == 0, pairs[:, 0], pairs[:, 1])
        send = jnp.where(bit == 0, pairs[:, 1], pairs[:, 0])
        pairs_list = [(i, i ^ step) for i in range(n)]
        if step >= 2:
            recv = lax.ppermute(send.astype(jnp.bfloat16), axis, pairs_list)
        else:
            recv = lax.ppermute(send, axis, pairs_list)
        if step * 2 >= n:
            return keep[0], recv[0]
        recv = recv.astype(jnp.float32)
        held = keep + recv
        step *= 2
    return held[0], jnp.zeros_like(held[0])


def make_local(n_dom, n_ka):
    def local(
        cell_coordinates_frac, site_strengths, miller_indices, occupied_site_tally, gaussian_spread
    ):
        channels = site_strengths.shape[0]
        n_local = cell_coordinates_frac.shape[1]
        atoms_total = n_local * n_dom
        live = jnp.arange(n_local) < occupied_site_tally[0]
        charge_live = jnp.where(live[None, :], site_strengths, jnp.zeros_like(site_strengths))
        cartesian_mode_vector = miller_indices.astype(jnp.float32)
        t = (
            cartesian_mode_vector[0][:, None] * cell_coordinates_frac[0][None, :]
            + cartesian_mode_vector[1][:, None] * cell_coordinates_frac[1][None, :]
            + cartesian_mode_vector[2][:, None] * cell_coordinates_frac[2][None, :]
        )
        cos_f, sin_f = turns_cos_sin(t)
        cos_table = cos_f.astype(jnp.bfloat16)
        sin_table = sin_f.astype(jnp.bfloat16)
        cos_table, sin_table = lax.optimization_barrier((cos_table, sin_table))
        tensor_product = (((1,), (1,)), ((), ()))
        s_cos = lax.dot_general(
            charge_live, cos_table, tensor_product, preferred_element_type=jnp.float32
        )
        s_sin = lax.dot_general(
            charge_live, sin_table, tensor_product, preferred_element_type=jnp.float32
        )
        s_both = butterfly_sum(jnp.stack([s_cos, s_sin], 0), n_dom, n_ka)
        cos_side, sin_side = reciprocal_filter_weight(
            s_both[0], s_both[1], cartesian_mode_vector, gaussian_spread, atoms_total
        )
        field = jnp.dot(cos_side, cos_table, preferred_element_type=jnp.float32)
        field = field + jnp.dot(sin_side, sin_table, preferred_element_type=jnp.float32)
        charge_f = charge_live.astype(jnp.float32)
        head = jnp.where(live[None, :], field[:channels], 0.0)
        force_rows = [
            jnp.sum(charge_f * field[channels * (1 + d) : channels * (2 + d)], 0, keepdims=True)
            for d in range(3)
        ]
        partial = jnp.concatenate([head] + force_rows, 0)
        rows = n_local // n_ka
        blocks = jnp.stack([partial[:, b * rows : (b + 1) * rows] for b in range(n_ka)], 0)
        own, other = halving_scatter(blocks, "ka", n_ka)
        potential = own[:channels] + other[:channels].astype(jnp.float32)
        forces = own[channels:] + other[channels:].astype(jnp.float32)
        return (potential, forces)

    return local


def solution(mesh):
    placed = (P(None, "dom"), P(None, "dom"), P(None, "ka"), P("dom"), P())
    return jax.shard_map(
        make_local(mesh.shape["dom"], mesh.shape["ka"]),
        mesh=mesh,
        in_specs=placed,
        out_specs=(P(None, ("dom", "ka")), P(None, ("dom", "ka"))),
        check_vma=False,
    )
```
